128 devices in a mesh: req: 16 (over z, x), exp: 8 (over y, core).
Axes of the slice: x: 4, y: 4, z: 4, core: 2. Of those that a mesh axis runs over, the one named last changes fastest.
Arguments:
- tokens: bfloat16 [12288, 2880], P(('req', 'exp')), may hold values from -6 to 6
- attn_gain: float32 [2880], replicated, may hold values from 0.5 to 8
- w_query: bfloat16 [2880, 4096], P(None, 'exp'), may hold values from -0.109375 to 0.109375
- key_weight: bfloat16 [2880, 512], P(None, 'exp'), may hold values from -0.109375 to 0.109375
- value_weight: bfloat16 [2880, 512], P(None, 'exp'), may hold values from -0.109375 to 0.109375
- sinks: float32 [64], P('exp'), may hold values from -1 to 3
- w_out: bfloat16 [4096, 2880], P('exp'), may hold values from -0.09375 to 0.09375
- ffn_gain: float32 [2880], replicated, may hold values from 0.25 to 1.75
- router: bfloat16 [2880, 32], replicated, may hold values from -0.109375 to 0.109375
- routes: int32 [12288, 4], P(('req', 'exp')), may hold values from 0 to 31, all different within a row; in each aligned block of 96 rows (0 to 95, 96 to 191, ...) at most 14 rows name the same one
- lengths: int32 [16, 6], P('req'), may hold values from 1 to 384, 768 in all within a row
- expert_gate: bfloat16 [128, 2880, 720], P(('req', 'exp')), may hold values from -0.109375 to 0.109375
- expert_up: bfloat16 [128, 2880, 720], P(('req', 'exp')), may hold values from -0.109375 to 0.109375
- expert_down: bfloat16 [128, 720, 2880], P(('req', 'exp')), may hold values from -0.109375 to 0.109375
Outputs:
- layer_out: bfloat16 [12288, 2880], P(('req', 'exp'))
The draws below stay inside these ranges and needn't reach their ends.
Inputs may be any that keep to these rules, and one draw needn't show every extreme that they name: `routes`: in the rows of one device no expert is named by more than 14 rows, a bound that some block reaches; a row names 4 different experts.
All inputs are finite; a program needn't handle non-finite values.
Results may differ from the reference program's by a relative error of at most 0.02.
The reference program's roundings to bfloat16 on the way count: a program that leaves them out, or rounds other values in their place, can miss the bound.
Values may be sent and summed in bfloat16 or wider, within the bound.
No kernel may reach another device: no remote copies, remote signals or barrier semaphores. Data moves between devices by JAX's collectives and lax.ppermute only.
A program may use at most 192 MiB of HBM per device.

```python
import math
import jax
import jax.numpy as jnp
import numpy as np
from jax import lax

MODEL_DIM = 2880
QUERY_HEADS = 64
KEY_VALUE_HEADS = 8
HEAD_DIM = 64
EXPERTS = 32
FF = 2880
TOPK = 4
TOK_DEV = 96
REQS = 6
SEQ = 768
TOKENS = 12288
LONGEST = 384
CAP = 14
SPLIT = 4
FF_DEV = 720
N_REQ = 16
N_EXP = 8
DEVICES = 128


def draw_attn_gain(key, part):
    return jax.random.uniform(key, (MODEL_DIM,), jnp.float32, 0.5, 1.5)


def shard_levels(stream_key, shape, pieces, low, largest):
    loudness, own = 1.0, jax.random.fold_in(stream_key, 6)
    for dim, blocks in pieces:
        heights = jnp.exp(jax.random.uniform(jax.random.fold_in(own, dim), (blocks,), jnp.float32, low / len(pieces), largest / len(pieces)))
        loudness = loudness * jnp.repeat(heights, shape[dim] // blocks).reshape([-1 if axis == dim else 1 for axis in range(len(shape))])
    return loudness


def profile(amount, total, most, skew):
    loads = [(1 << 20) // math.isqrt(rank ** skew) + 1 for rank in range(2, amount + 1)]
    rest, holding = total - most - (amount - 1), [1] * (amount - 1)
    while rest > 0:
        candidates = [i for i in range(amount - 1) if holding[i] < most]
        whole, budget = sum([loads[i] for i in candidates]), rest
        for i in candidates:
            extra = min(most - holding[i], max(1, budget * loads[i] // whole), rest)
            holding[i] = holding[i] + extra
            rest = rest - extra
    return np.array([most] + holding)


def uneven(rng, amount, total, reach, lean):
    if amount == 2:
        one = jax.random.randint(rng, (), max(1, total - reach), min(reach, total - 1) + 1)
        return jnp.stack([one, total - one])
    tallies = jnp.asarray(profile(amount, total, reach, lean), jnp.int32)
    couples = (amount - 1) // 2
    giver, sink = tallies[1:1 + 2 * couples:2], tallies[2:2 + 2 * couples:2]
    slack = jnp.minimum(giver - 1, reach - sink)
    shifted = jax.random.randint(jax.random.fold_in(rng, 1), (couples,), 0, 1 << 20) % (slack + 1)
    tallies = tallies.at[1:1 + 2 * couples:2].set(giver - shifted).at[2:2 + 2 * couples:2].set(sink + shifted)
    return tallies[jax.random.permutation(jax.random.fold_in(rng, 2), amount)]


def shared_out(rng, own, number, rows, count, top, bound, skew):
    sequence = jax.random.permutation(rng, count)
    packed, usual = shares(count, rows * top, bound, skew, True), shares(count, rows * top, bound, skew, False)
    places = jnp.arange(count)

    def named(tallies, rotation):
        used = int((tallies > 0).sum())
        fixed = max(1, used // 4)
        shifted = fixed + (places - fixed + rotation * (used - fixed)) % max(1, count - fixed)
        return jnp.zeros((count,), jnp.int32).at[sequence[jnp.where(places < fixed, places, shifted)]].set(jnp.asarray(tallies, jnp.int32))

    tallies = jnp.where(number % 4 == 0, named(packed, number // 4), named(usual, number - number // 4 - 1))
    mixed = jax.random.permutation(jax.random.fold_in(own, 3), count)
    giver, taker = mixed[0:count // 2 * 2:2], mixed[1:count // 2 * 2:2]
    margin = jnp.minimum(tallies[giver] - 1, bound - tallies[taker]) // 2
    margin = jnp.where((giver == sequence[0]) | (taker == sequence[0]) | (tallies[taker] == 0), 0, jnp.maximum(margin, 0))
    shifted = jax.random.randint(jax.random.fold_in(own, 4), (count // 2,), 0, 1 << 20) % (margin + 1)
    tallies = tallies.at[giver].add(-shifted).at[taker].add(shifted)
    labels = jnp.searchsorted(jnp.cumsum(tallies), jnp.arange(rows * top), side="right").astype(jnp.int32)
    table = labels.reshape(top, rows).T
    table = table[jax.random.permutation(jax.random.fold_in(own, 1), rows)]
    rotation = jax.random.randint(jax.random.fold_in(own, 2), (rows, 1), 0, top)
    return jnp.take_along_axis(table, (jnp.arange(top)[None, :] + rotation) % top, axis=1)


def shares(amount, total, bound, slope, full):
    weights = [(1 << 20) // math.isqrt(rank ** slope) + 1 for rank in range(1, amount + 1)]
    largest = bound if full else min(bound, max(-(-total // amount), total * weights[0] // sum(weights)))
    least = 1 if total - largest >= amount - 1 else 0
    holding, spare = [largest] + [least] * (amount - 1), total - largest - least * (amount - 1)
    while spare > 0:
        free = [i for i in range(1, amount) if holding[i] < largest] or [i for i in range(1, amount) if holding[i] < bound]
        whole, remaining = sum([weights[i] for i in free]), spare
        for i in free:
            extra = min(bound - holding[i], max(1, remaining * weights[i] // whole), spare)
            holding[i] = holding[i] + extra
            spare = spare - extra
    return np.array(holding)


def bell_draw(key, shape, width, bound, split=(), held_as=jnp.bfloat16):
    array = width * jax.random.normal(key, shape, jnp.float32)
    if split:
        array = array * shard_levels(key, shape, split, -0.22, 0.18)
    return jnp.clip(array, -bound, bound).astype(held_as)


def setup_inputs(seed: int = 0) -> dict:
    arg_keys = jax.random.split(jax.random.key(seed), 15)
    tokens = bell_draw(arg_keys[0], (TOKENS, MODEL_DIM), 1.0, 6.0, ((0, 128),))
    attn_gain = draw_attn_gain(jax.random.fold_in(arg_keys[14], 71), 0)
    w_query = bell_draw(arg_keys[2], (MODEL_DIM, QUERY_HEADS * HEAD_DIM), MODEL_DIM ** -0.5, 0.109375, ((1, 8),))
    key_weight = bell_draw(arg_keys[3], (MODEL_DIM, KEY_VALUE_HEADS * HEAD_DIM), MODEL_DIM ** -0.5, 0.109375, ((1, 8),))
    value_weight = bell_draw(arg_keys[4], (MODEL_DIM, KEY_VALUE_HEADS * HEAD_DIM), MODEL_DIM ** -0.5, 0.109375, ((1, 8),))
    sinks = jnp.clip(-1.0 + 4.0 * jax.random.uniform(arg_keys[5], (QUERY_HEADS,), jnp.float32) ** shard_levels(arg_keys[5], (QUERY_HEADS,), ((0, 8),), -0.2, 0.2), -1.0, 3.0)
    w_out = bell_draw(arg_keys[6], (QUERY_HEADS * HEAD_DIM, MODEL_DIM), (QUERY_HEADS * HEAD_DIM) ** -0.5, 0.09375, ((0, 8),))
    ffn_gain = jnp.clip(1.0 + 0.15 * jax.random.normal(arg_keys[7], (MODEL_DIM,), jnp.float32), 0.25, 1.75)
    router = bell_draw(arg_keys[8], (MODEL_DIM, EXPERTS), MODEL_DIM ** -0.5, 0.109375)
    routes_keys = jax.random.split(jax.random.fold_in(arg_keys[9], 1), TOKENS // TOK_DEV)
    routes_turns = jax.random.permutation(jax.random.fold_in(arg_keys[9], 3), TOKENS // TOK_DEV)
    routes = jax.vmap(lambda own, number: shared_out(jax.random.fold_in(arg_keys[9], 2), own, number, TOK_DEV, EXPERTS, TOPK, CAP, 2))(routes_keys, routes_turns).reshape((TOKENS, TOPK))
    lengths = jax.vmap(lambda own: uneven(own, REQS, SEQ, LONGEST, 2))(jax.random.split(arg_keys[10], N_REQ)).reshape((N_REQ, REQS)).astype(jnp.int32)
    expert_gate = bell_draw(arg_keys[11], (SPLIT * EXPERTS, MODEL_DIM, FF_DEV), MODEL_DIM ** -0.5, 0.109375, ((0, 128),))
    expert_up = bell_draw(arg_keys[12], (SPLIT * EXPERTS, MODEL_DIM, FF_DEV), MODEL_DIM ** -0.5, 0.109375, ((0, 128),))
    expert_down = bell_draw(arg_keys[13], (SPLIT * EXPERTS, FF_DEV, MODEL_DIM), FF ** -0.5, 0.109375, ((0, 128),))
    return dict(tokens=tokens, attn_gain=attn_gain, w_query=w_query, key_weight=key_weight, value_weight=value_weight, sinks=sinks, w_out=w_out, ffn_gain=ffn_gain, router=router, routes=routes, lengths=lengths, expert_gate=expert_gate, expert_up=expert_up, expert_down=expert_down)


def rms_norm(value_rows, gain):
    mean_sq = lax.optimization_barrier(jnp.mean(value_rows * value_rows, axis=-1, keepdims=True))
    return value_rows * lax.rsqrt(mean_sq + 1e-05) * gain

def seg_and_pos(lens, item_count):
    ends = jnp.cumsum(lens).astype(jnp.int32)
    starts = (ends - lens).astype(jnp.int32)
    position = jnp.arange(item_count, dtype=jnp.int32)
    member = ((position[:, None] >= starts[None, :]) & (position[:, None] < ends[None, :])).astype(jnp.int32)
    segment = lax.optimization_barrier(jnp.sum(member * jnp.arange(lens.shape[0], dtype=jnp.int32)[None, :], axis=1))
    offset = position - lax.optimization_barrier(jnp.sum(member * starts[None, :], axis=1))
    return (segment, offset)

def rotate(value_rows, offset):
    half = value_rows.shape[-1] // 2
    freqs = jnp.exp(-(2.0 * jnp.arange(half, dtype=jnp.float32) / value_rows.shape[-1]) * jnp.log(jnp.float32(150000.0)))
    angle = offset.astype(jnp.float32)[:, None] * freqs[None, :]
    cosine = jnp.cos(angle)[:, None, :]
    sine = jnp.sin(angle)[:, None, :]
    first = value_rows[..., :half]
    second = value_rows[..., half:]
    return jnp.concatenate([first * cosine - second * sine, second * cosine + first * sine], axis=-1)

def attend_group(group_tokens, lens, attn_gain, w_query, key_weight, value_weight, sinks):
    item_count = group_tokens.shape[0]
    segment, offset = seg_and_pos(lens, item_count)
    normed_input = rms_norm(group_tokens.astype(jnp.float32), attn_gain).astype(jnp.bfloat16)
    query_rows = jnp.dot(normed_input, w_query, preferred_element_type=jnp.float32).reshape(item_count, QUERY_HEADS, HEAD_DIM)
    key_rows = jnp.dot(normed_input, key_weight, preferred_element_type=jnp.float32).reshape(item_count, KEY_VALUE_HEADS, HEAD_DIM)
    value_rows = jnp.dot(normed_input, value_weight, preferred_element_type=jnp.float32).reshape(item_count, KEY_VALUE_HEADS, HEAD_DIM)
    query_rows = rotate(query_rows, offset).astype(jnp.bfloat16)
    key_rows = rotate(key_rows, offset).astype(jnp.bfloat16)
    value_rows = value_rows.astype(jnp.bfloat16)
    head_group = QUERY_HEADS // KEY_VALUE_HEADS
    grouped_heads = query_rows.reshape(item_count, KEY_VALUE_HEADS, head_group, HEAD_DIM).astype(jnp.float32)
    scores = jnp.einsum('qcgd,kcd->cgqk', grouped_heads, key_rows.astype(jnp.float32)) * HEAD_DIM ** (-0.5)
    position = jnp.arange(item_count, dtype=jnp.int32)
    allowed = (segment[:, None] == segment[None, :]) & (position[None, :] <= position[:, None])
    sink_score_logit = sinks.reshape(KEY_VALUE_HEADS, head_group, 1, 1)
    masked = jnp.where(allowed[None, None], scores, -jnp.inf)
    top = jnp.maximum(lax.optimization_barrier(jnp.max(masked, axis=-1, keepdims=True)), sink_score_logit)
    expo = jnp.where(allowed[None, None], jnp.exp(scores - top), 0.0)
    denom = lax.optimization_barrier(jnp.sum(expo, axis=-1, keepdims=True)) + jnp.exp(sink_score_logit - top)
    probs = (expo / denom).astype(jnp.bfloat16)
    attended = jnp.einsum('cgqk,kcd->qcgd', probs.astype(jnp.float32), value_rows.astype(jnp.float32))
    return attended.reshape(item_count, QUERY_HEADS * HEAD_DIM).astype(jnp.bfloat16)

def reference(tokens, attn_gain, w_query, key_weight, value_weight, sinks, w_out, ffn_gain, router, routes, lengths, expert_gate, expert_up, expert_down):

    def one_group(pair):
        return attend_group(pair[0], pair[1], attn_gain, w_query, key_weight, value_weight, sinks)
    attended = lax.map(one_group, (tokens.reshape(N_REQ, SEQ, MODEL_DIM), lengths)).reshape(TOKENS, QUERY_HEADS * HEAD_DIM)
    block = QUERY_HEADS * HEAD_DIM // N_EXP
    attended_parts = attended.reshape(TOKENS, N_EXP, block).transpose(1, 0, 2)
    out_parts = w_out.reshape(N_EXP, block, MODEL_DIM)

    def add_part(total, pair):
        term = jnp.dot(pair[0], pair[1], preferred_element_type=jnp.float32).astype(jnp.bfloat16)
        term = lax.optimization_barrier(term)
        return (total + term.astype(jnp.float32), None)
    attn_sum, _ = lax.scan(add_part, jnp.zeros((TOKENS, MODEL_DIM), jnp.float32), (attended_parts, out_parts))
    residual = (tokens.astype(jnp.float32) + attn_sum).astype(jnp.bfloat16)
    normed2 = rms_norm(residual.astype(jnp.float32), ffn_gain).astype(jnp.bfloat16)
    logits = jnp.dot(normed2, router, preferred_element_type=jnp.float32)
    picked = jnp.take_along_axis(logits, routes, axis=1)
    weights = jax.nn.softmax(picked, axis=-1)
    flat_routes = routes.reshape(-1)
    flat_weights = weights.reshape(-1)
    rows_max = DEVICES * CAP
    gate_all = expert_gate.reshape(EXPERTS, SPLIT, MODEL_DIM, FF_DEV)
    up_all = expert_up.reshape(EXPERTS, SPLIT, MODEL_DIM, FF_DEV)
    down_all = expert_down.reshape(EXPERTS, SPLIT, FF_DEV, MODEL_DIM)

    def expert_step(total, inputs):
        expert_id, gate_w, up_w, down_w = inputs
        sort_key = (flat_routes != expert_id).astype(jnp.int32)
        order = jnp.argsort(sort_key, stable=True)[:rows_max].astype(jnp.int32)
        valid = (flat_routes[order] == expert_id).astype(jnp.float32)
        token_rows = order // TOPK
        rows = normed2[token_rows]
        summed = jnp.zeros((rows_max, MODEL_DIM), jnp.float32)
        for slice_index in range(SPLIT):
            gate = jnp.dot(rows, gate_w[slice_index], preferred_element_type=jnp.float32)
            up_val = jnp.dot(rows, up_w[slice_index], preferred_element_type=jnp.float32)
            hidden = ((up_val + 1.0) * gate * jax.nn.sigmoid(1.702 * gate)).astype(jnp.bfloat16)
            slice_out = jnp.dot(hidden, down_w[slice_index], preferred_element_type=jnp.float32).astype(jnp.bfloat16)
            slice_out = lax.optimization_barrier(slice_out)
            summed = summed + slice_out.astype(jnp.float32)
        scaled = summed * (flat_weights[order] * valid)[:, None]
        return (total.at[token_rows].add(scaled), None)
    moe_sum, _ = lax.scan(expert_step, jnp.zeros((TOKENS, MODEL_DIM), jnp.float32), (jnp.arange(EXPERTS, dtype=jnp.int32), gate_all, up_all, down_all))
    return (residual.astype(jnp.float32) + moe_sum).astype(jnp.bfloat16)
```

```python
import jax
import jax.numpy as jnp
from jax import lax
from jax.sharding import PartitionSpec as P

QUERY_HEADS = 64
KEY_VALUE_HEADS = 8
HEAD_DIM = 64
EXPERTS = 32
TOPK = 4
CAP = 14


def rms_norm(value_rows, gain):
    mean_sq = jnp.mean(value_rows * value_rows, axis=-1, keepdims=True)
    return value_rows * lax.rsqrt(mean_sq + 1e-05) * gain


def rotate(value_rows, offset):
    half = value_rows.shape[-1] // 2
    freqs = jnp.exp(
        -(2.0 * jnp.arange(half, dtype=jnp.float32) / value_rows.shape[-1])
        * jnp.log(jnp.float32(150000.0))
    )
    angle = offset.astype(jnp.float32)[:, None] * freqs[None, :]
    cosine = jnp.cos(angle)[:, None, :]
    sine = jnp.sin(angle)[:, None, :]
    first = value_rows[..., :half]
    second = value_rows[..., half:]
    return jnp.concatenate(
        [first * cosine - second * sine, second * cosine + first * sine], axis=-1
    )


def per_device(
    tokens,
    attn_gain,
    w_query,
    key_weight,
    value_weight,
    sinks,
    w_out,
    ffn_gain,
    router,
    routes,
    lengths,
    expert_gate,
    expert_up,
    expert_down,
):
    tok_rows = tokens.shape[0]
    model_width = tokens.shape[1]
    local_heads = w_query.shape[1] // HEAD_DIM
    local_kv = key_weight.shape[1] // HEAD_DIM
    head_group = QUERY_HEADS // KEY_VALUE_HEADS
    normed_input = rms_norm(tokens.astype(jnp.float32), attn_gain).astype(jnp.bfloat16)
    by_chip = lax.all_gather(normed_input, "y", axis=0, tiled=False)
    piece = lax.all_gather(by_chip, "c", axis=1, tiled=True).reshape(-1, model_width)
    projected = jnp.concatenate(
        [
            jnp.dot(piece, w_query, preferred_element_type=jnp.float32),
            jnp.dot(piece, key_weight, preferred_element_type=jnp.float32),
            jnp.dot(piece, value_weight, preferred_element_type=jnp.float32),
        ],
        axis=1,
    )
    item_count = projected.shape[0]
    lens = lengths[0]
    ends = jnp.cumsum(lens)
    starts = ends - lens
    position = jnp.arange(item_count, dtype=jnp.int32)
    member = ((position[:, None] >= starts[None, :]) & (position[:, None] < ends[None, :])).astype(
        jnp.int32
    )
    segment = jnp.sum(member * jnp.arange(lens.shape[0], dtype=jnp.int32)[None, :], axis=1)
    offset = position - jnp.sum(member * starts[None, :], axis=1)
    q_width = local_heads * HEAD_DIM
    kv_width = local_kv * HEAD_DIM
    query_rows = rotate(
        projected[:, :q_width].reshape(item_count, local_heads, HEAD_DIM), offset
    ).astype(jnp.bfloat16)
    key_rows = rotate(
        projected[:, q_width : q_width + kv_width].reshape(item_count, local_kv, HEAD_DIM), offset
    ).astype(jnp.bfloat16)
    value_rows = (
        projected[:, q_width + kv_width :]
        .reshape(item_count, local_kv, HEAD_DIM)
        .astype(jnp.bfloat16)
    )
    grouped_heads = query_rows.reshape(item_count, local_kv, head_group, HEAD_DIM)
    scores = jnp.einsum(
        "qcgd,kcd->cgqk", grouped_heads, key_rows, preferred_element_type=jnp.float32
    ) * HEAD_DIM ** (-0.5)
    allowed = (segment[:, None] == segment[None, :]) & (position[None, :] <= position[:, None])
    sink_score_logit = sinks.reshape(local_kv, head_group, 1, 1)
    masked = jnp.where(allowed[None, None], scores, -jnp.inf)
    top = jnp.maximum(jnp.max(masked, axis=-1, keepdims=True), sink_score_logit)
    expo = jnp.where(allowed[None, None], jnp.exp(scores - top), 0.0)
    denom = jnp.sum(expo, axis=-1, keepdims=True) + jnp.exp(sink_score_logit - top)
    probs = (expo / denom).astype(jnp.bfloat16)
    attended = jnp.einsum("cgqk,kcd->qcgd", probs, value_rows, preferred_element_type=jnp.float32)
    attended = attended.reshape(item_count, q_width).astype(jnp.bfloat16)
    head_term = jnp.dot(attended, w_out, preferred_element_type=jnp.float32).astype(jnp.bfloat16)
    n_y = lax.axis_size("y")
    n_c = lax.axis_size("c")
    head_term = head_term.reshape(n_y, n_c, tok_rows, model_width).transpose(1, 0, 2, 3)
    on_chip = lax.psum_scatter(head_term, "c", scatter_dimension=0, tiled=True)
    attn_sum = lax.psum_scatter(
        on_chip.reshape(n_y, tok_rows, model_width), "y", scatter_dimension=0, tiled=True
    ).reshape(tok_rows, model_width).astype(jnp.float32)
    residual = (tokens.astype(jnp.float32) + attn_sum).astype(jnp.bfloat16)
    normed2 = rms_norm(residual.astype(jnp.float32), ffn_gain).astype(jnp.bfloat16)
    logits = jnp.dot(normed2, router, preferred_element_type=jnp.float32)
    picked = jnp.take_along_axis(logits, routes, axis=1)
    weights = jax.nn.softmax(picked, axis=-1)
    flat_routes = routes.reshape(-1)
    expert_ids = jnp.arange(EXPERTS, dtype=jnp.int32)
    onehot_route = (flat_routes[:, None] == expert_ids[None, :]).astype(jnp.int32)
    rank = jnp.cumsum(onehot_route, axis=0) - 1
    slot_rank = jnp.sum(onehot_route * rank, axis=1)
    flat_slot = flat_routes * CAP + slot_rank
    slot_ids = jnp.arange(EXPERTS * CAP, dtype=jnp.int32)
    dispatch_table = (slot_ids[:, None] == flat_slot[None, :]).astype(jnp.bfloat16)
    repeated = jnp.repeat(normed2, TOPK, axis=0)
    packed = jnp.dot(dispatch_table, repeated, preferred_element_type=jnp.float32).astype(
        jnp.bfloat16
    )
    halves = n_y // (EXPERTS // lax.axis_size("req"))
    send_rows = jnp.broadcast_to(
        packed.reshape(EXPERTS, 1, CAP, model_width), (EXPERTS, halves, CAP, model_width)
    ).reshape(EXPERTS * halves, CAP, model_width)
    received = lax.all_to_all(send_rows, ("req", "y"), split_axis=0, concat_axis=0, tiled=True)
    both = lax.all_gather(received, "c", axis=0, tiled=False)
    flat_rows = both.reshape(-1, model_width)
    gate = jnp.dot(flat_rows, expert_gate[0], preferred_element_type=jnp.float32)
    up_val = jnp.dot(flat_rows, expert_up[0], preferred_element_type=jnp.float32)
    hidden = ((up_val + 1.0) * gate * jax.nn.sigmoid(1.702 * gate)).astype(jnp.bfloat16)
    slice_out = jnp.dot(hidden, expert_down[0], preferred_element_type=jnp.float32).astype(
        jnp.bfloat16
    )
    swapped = lax.all_to_all(
        slice_out.reshape(both.shape), "c", split_axis=0, concat_axis=0, tiled=True
    )
    chip_sum = swapped.astype(jnp.float32).sum(axis=0).astype(jnp.bfloat16)
    returned = lax.all_to_all(chip_sum, ("req", "y"), split_axis=0, concat_axis=0, tiled=True)
    summed = returned.astype(jnp.float32).reshape(EXPERTS, halves, CAP, model_width).sum(axis=1)
    summed = summed.reshape(EXPERTS * CAP, model_width)
    picked_rows = jnp.take(summed, flat_slot, axis=0).reshape(tok_rows, TOPK, model_width)
    moe_sum = jnp.sum(weights[:, :, None] * picked_rows, axis=1)
    return (residual.astype(jnp.float32) + moe_sum).astype(jnp.bfloat16)


def solution(mesh):
    n_req, n_exp = mesh.devices.shape
    fine = jax.sharding.Mesh(mesh.devices.reshape(n_req, n_exp // 2, 2), ("req", "y", "c"))
    tok = ("req", "y", "c")
    return jax.shard_map(
        per_device,
        mesh=fine,
        in_specs=(
            P(tok, None),
            P(),
            P(None, ("y", "c")),
            P(None, ("y", "c")),
            P(None, ("y", "c")),
            P(("y", "c")),
            P(("y", "c"), None),
            P(),
            P(),
            P(tok, None),
            P("req", None),
            P(tok, None, None),
            P(tok, None, None),
            P(tok, None, None),
        ),
        out_specs=P(tok, None),
        check_vma=False,
    )
```

```python
import jax
import jax.numpy as jnp
from jax import lax
from jax.sharding import PartitionSpec as P

QUERY_HEADS = 64
KEY_VALUE_HEADS = 8
HEAD_DIM = 64
EXPERTS = 32
TOPK = 4
CAP = 14
ROWS = 16


def rms_norm(value_rows, gain):
    mean_sq = jnp.mean(value_rows * value_rows, axis=-1, keepdims=True)
    return value_rows * lax.rsqrt(mean_sq + 1e-05) * gain


def rotate(value_rows, offset):
    half = value_rows.shape[-1] // 2
    freqs = jnp.exp(
        -(2.0 * jnp.arange(half, dtype=jnp.float32) / value_rows.shape[-1])
        * jnp.log(jnp.float32(150000.0))
    )
    angle = offset.astype(jnp.float32)[:, None] * freqs[None, :]
    cosine = jnp.cos(angle)[:, None, :]
    sine = jnp.sin(angle)[:, None, :]
    first = value_rows[..., :half]
    second = value_rows[..., half:]
    return jnp.concatenate(
        [first * cosine - second * sine, second * cosine + first * sine], axis=-1
    )


def per_device(
    tokens,
    attn_gain,
    w_query,
    key_weight,
    value_weight,
    sinks,
    w_out,
    ffn_gain,
    router,
    routes,
    lengths,
    expert_gate,
    expert_up,
    expert_down,
):
    tok_rows = tokens.shape[0]
    model_width = tokens.shape[1]
    local_heads = w_query.shape[1] // HEAD_DIM
    local_kv = key_weight.shape[1] // HEAD_DIM
    head_group = QUERY_HEADS // KEY_VALUE_HEADS
    normed_input = rms_norm(tokens.astype(jnp.float32), attn_gain).astype(jnp.bfloat16)
    piece = lax.all_gather(normed_input, ("y", "c"), axis=0, tiled=True)
    projected = jnp.concatenate(
        [
            jnp.dot(piece, w_query, preferred_element_type=jnp.float32),
            jnp.dot(piece, key_weight, preferred_element_type=jnp.float32),
            jnp.dot(piece, value_weight, preferred_element_type=jnp.float32),
        ],
        axis=1,
    )
    item_count = projected.shape[0]
    lens = lengths[0]
    ends = jnp.cumsum(lens)
    starts = ends - lens
    position = jnp.arange(item_count, dtype=jnp.int32)
    member = ((position[:, None] >= starts[None, :]) & (position[:, None] < ends[None, :])).astype(
        jnp.int32
    )
    segment = jnp.sum(member * jnp.arange(lens.shape[0], dtype=jnp.int32)[None, :], axis=1)
    offset = position - jnp.sum(member * starts[None, :], axis=1)
    q_width = local_heads * HEAD_DIM
    kv_width = local_kv * HEAD_DIM
    query_rows = rotate(
        projected[:, :q_width].reshape(item_count, local_heads, HEAD_DIM), offset
    ).astype(jnp.bfloat16)
    key_rows = rotate(
        projected[:, q_width : q_width + kv_width].reshape(item_count, local_kv, HEAD_DIM), offset
    ).astype(jnp.bfloat16)
    value_rows = (
        projected[:, q_width + kv_width :]
        .reshape(item_count, local_kv, HEAD_DIM)
        .astype(jnp.bfloat16)
    )
    grouped_heads = query_rows.reshape(item_count, local_kv, head_group, HEAD_DIM)
    scores = jnp.einsum(
        "qcgd,kcd->cgqk", grouped_heads, key_rows, preferred_element_type=jnp.float32
    ) * HEAD_DIM ** (-0.5)
    allowed = (segment[:, None] == segment[None, :]) & (position[None, :] <= position[:, None])
    sink_score_logit = sinks.reshape(local_kv, head_group, 1, 1)
    masked = jnp.where(allowed[None, None], scores, -jnp.inf)
    top = jnp.maximum(jnp.max(masked, axis=-1, keepdims=True), sink_score_logit)
    expo = jnp.where(allowed[None, None], jnp.exp(scores - top), 0.0)
    denom = jnp.sum(expo, axis=-1, keepdims=True) + jnp.exp(sink_score_logit - top)
    probs = (expo / denom).astype(jnp.bfloat16)
    attended = jnp.einsum("cgqk,kcd->qcgd", probs, value_rows, preferred_element_type=jnp.float32)
    attended = attended.reshape(item_count, q_width).astype(jnp.bfloat16)
    attn_sum = lax.psum_scatter(
        jnp.dot(attended, w_out, preferred_element_type=jnp.float32).astype(jnp.bfloat16),
        ("y", "c"),
        scatter_dimension=0,
        tiled=True,
    ).astype(jnp.float32)
    residual = (tokens.astype(jnp.float32) + attn_sum).astype(jnp.bfloat16)
    normed2 = rms_norm(residual.astype(jnp.float32), ffn_gain).astype(jnp.bfloat16)
    logits = jnp.dot(normed2, router, preferred_element_type=jnp.float32)
    picked = jnp.take_along_axis(logits, routes, axis=1)
    weights = jax.nn.softmax(picked, axis=-1)
    flat_routes = routes.reshape(-1)
    expert_ids = jnp.arange(EXPERTS, dtype=jnp.int32)
    onehot_route = (flat_routes[:, None] == expert_ids[None, :]).astype(jnp.int32)
    rank = jnp.cumsum(onehot_route, axis=0) - 1
    slot_rank = jnp.sum(onehot_route * rank, axis=1)
    n_y = lax.axis_size("y")
    halves = n_y // (EXPERTS // lax.axis_size("req"))
    pos = (flat_routes[:, None] * halves + jnp.arange(halves, dtype=jnp.int32)[None, :]) * ROWS
    pos = (pos + slot_rank[:, None]).reshape(tok_rows, TOPK, halves)
    row_ids = jnp.arange(EXPERTS * halves * ROWS, dtype=jnp.int32)
    match = pos[:, :, :, None] == row_ids[None, None, None, :]
    dispatch_table = jnp.any(match, axis=(1, 2)).T.astype(jnp.bfloat16)
    send_rows = jnp.dot(dispatch_table, normed2, preferred_element_type=jnp.float32).astype(
        jnp.bfloat16
    ).reshape(EXPERTS * halves, ROWS, model_width)
    combine = jnp.sum(jnp.where(match, weights[:, :, None, None], 0.0), axis=(1, 2))
    received = lax.all_to_all(send_rows, ("req", "y"), split_axis=0, concat_axis=0, tiled=True)
    swap = [(0, 1), (1, 0)]
    sibling_rows = lax.ppermute(received, "c", perm=swap)

    def expert_slice(rows):
        flat = rows.reshape(-1, model_width)
        gate = jnp.dot(flat, expert_gate[0], preferred_element_type=jnp.float32)
        up_val = jnp.dot(flat, expert_up[0], preferred_element_type=jnp.float32)
        hidden = ((up_val + 1.0) * gate * jax.nn.sigmoid(1.702 * gate)).astype(jnp.bfloat16)
        return jnp.dot(hidden, expert_down[0], preferred_element_type=jnp.float32).astype(
            jnp.bfloat16
        )

    own_out = expert_slice(received)
    sibling_out = expert_slice(sibling_rows)
    from_sibling = lax.ppermute(sibling_out, "c", perm=swap)
    chip_sum = (own_out.astype(jnp.float32) + from_sibling.astype(jnp.float32)).astype(jnp.bfloat16)
    returned = lax.all_to_all(
        chip_sum.reshape(received.shape), ("req", "y"), split_axis=0, concat_axis=0, tiled=True
    ).reshape(-1, model_width)
    combine_hi = combine.astype(jnp.bfloat16)
    combine_lo = (combine - combine_hi.astype(jnp.float32)).astype(jnp.bfloat16)
    moe_sum = jnp.dot(combine_hi, returned, preferred_element_type=jnp.float32) + jnp.dot(
        combine_lo, returned, preferred_element_type=jnp.float32
    )
    return (residual.astype(jnp.float32) + moe_sum).astype(jnp.bfloat16)


def solution(mesh):
    n_req, n_exp = mesh.devices.shape
    fine = jax.sharding.Mesh(mesh.devices.reshape(n_req, n_exp // 2, 2), ("req", "y", "c"))
    tok = ("req", "y", "c")
    return jax.shard_map(
        per_device,
        mesh=fine,
        in_specs=(
            P(tok, None),
            P(),
            P(None, ("y", "c")),
            P(None, ("y", "c")),
            P(None, ("y", "c")),
            P(("y", "c")),
            P(("y", "c"), None),
            P(),
            P(),
            P(tok, None),
            P("req", None),
            P(tok, None, None),
            P(tok, None, None),
            P(tok, None, None),
        ),
        out_specs=P(tok, None),
        check_vma=False,
    )
```

```python
import jax
import jax.numpy as jnp
from jax import lax
from jax.sharding import PartitionSpec as P

QUERY_HEADS = 64
KEY_VALUE_HEADS = 8
HEAD_DIM = 64
EXPERTS = 32
TOPK = 4
CAP = 14
ROWS = 16
CHUNK_ROWS = 8


def rms_norm(value_rows, gain):
    mean_sq = jnp.mean(value_rows * value_rows, axis=-1, keepdims=True)
    return value_rows * lax.rsqrt(mean_sq + 1e-05) * gain


def rotate(value_rows, offset):
    half = value_rows.shape[-1] // 2
    freqs = jnp.exp(
        -(2.0 * jnp.arange(half, dtype=jnp.float32) / value_rows.shape[-1])
        * jnp.log(jnp.float32(150000.0))
    )
    angle = offset.astype(jnp.float32)[:, None] * freqs[None, :]
    cosine = jnp.cos(angle)[:, None, :]
    sine = jnp.sin(angle)[:, None, :]
    first = value_rows[..., :half]
    second = value_rows[..., half:]
    return jnp.concatenate(
        [first * cosine - second * sine, second * cosine + first * sine], axis=-1
    )


def per_device(
    tokens,
    attn_gain,
    w_query,
    key_weight,
    value_weight,
    sinks,
    w_out,
    ffn_gain,
    router,
    routes,
    lengths,
    expert_gate,
    expert_up,
    expert_down,
):
    tok_rows = tokens.shape[0]
    model_width = tokens.shape[1]
    local_heads = w_query.shape[1] // HEAD_DIM
    local_kv = key_weight.shape[1] // HEAD_DIM
    head_group = QUERY_HEADS // KEY_VALUE_HEADS
    normed_input = rms_norm(tokens.astype(jnp.float32), attn_gain).astype(jnp.bfloat16)
    piece = lax.all_gather(normed_input, ("y", "c"), axis=0, tiled=True)
    projected = jnp.concatenate(
        [
            jnp.dot(piece, w_query, preferred_element_type=jnp.float32),
            jnp.dot(piece, key_weight, preferred_element_type=jnp.float32),
            jnp.dot(piece, value_weight, preferred_element_type=jnp.float32),
        ],
        axis=1,
    )
    item_count = projected.shape[0]
    lens = lengths[0]
    ends = jnp.cumsum(lens)
    starts = ends - lens
    position = jnp.arange(item_count, dtype=jnp.int32)
    member = ((position[:, None] >= starts[None, :]) & (position[:, None] < ends[None, :])).astype(
        jnp.int32
    )
    segment = jnp.sum(member * jnp.arange(lens.shape[0], dtype=jnp.int32)[None, :], axis=1)
    offset = position - jnp.sum(member * starts[None, :], axis=1)
    q_width = local_heads * HEAD_DIM
    kv_width = local_kv * HEAD_DIM
    query_rows = rotate(
        projected[:, :q_width].reshape(item_count, local_heads, HEAD_DIM), offset
    ).astype(jnp.bfloat16)
    key_rows = rotate(
        projected[:, q_width : q_width + kv_width].reshape(item_count, local_kv, HEAD_DIM), offset
    ).astype(jnp.bfloat16)
    value_rows = (
        projected[:, q_width + kv_width :]
        .reshape(item_count, local_kv, HEAD_DIM)
        .astype(jnp.bfloat16)
    )
    grouped_heads = query_rows.reshape(item_count, local_kv, head_group, HEAD_DIM)
    scores = jnp.einsum(
        "qcgd,kcd->cgqk", grouped_heads, key_rows, preferred_element_type=jnp.float32
    ) * HEAD_DIM ** (-0.5)
    allowed = (segment[:, None] == segment[None, :]) & (position[None, :] <= position[:, None])
    sink_score_logit = sinks.reshape(local_kv, head_group, 1, 1)
    masked = jnp.where(allowed[None, None], scores, -jnp.inf)
    top = jnp.maximum(jnp.max(masked, axis=-1, keepdims=True), sink_score_logit)
    expo = jnp.where(allowed[None, None], jnp.exp(scores - top), 0.0)
    denom = jnp.sum(expo, axis=-1, keepdims=True) + jnp.exp(sink_score_logit - top)
    probs = (expo / denom).astype(jnp.bfloat16)
    attended = jnp.einsum("cgqk,kcd->qcgd", probs, value_rows, preferred_element_type=jnp.float32)
    attended = attended.reshape(item_count, q_width).astype(jnp.bfloat16)
    attn_sum = lax.psum_scatter(
        jnp.dot(attended, w_out, preferred_element_type=jnp.float32).astype(jnp.bfloat16),
        ("y", "c"),
        scatter_dimension=0,
        tiled=True,
    ).astype(jnp.float32)
    residual = (tokens.astype(jnp.float32) + attn_sum).astype(jnp.bfloat16)
    normed2 = rms_norm(residual.astype(jnp.float32), ffn_gain).astype(jnp.bfloat16)
    logits = jnp.dot(normed2, router, preferred_element_type=jnp.float32)
    picked = jnp.take_along_axis(logits, routes, axis=1)
    weights = jax.nn.softmax(picked, axis=-1)
    flat_routes = routes.reshape(-1)
    expert_ids = jnp.arange(EXPERTS, dtype=jnp.int32)
    onehot_route = (flat_routes[:, None] == expert_ids[None, :]).astype(jnp.int32)
    rank = jnp.cumsum(onehot_route, axis=0) - 1
    slot_rank = jnp.sum(onehot_route * rank, axis=1)
    n_y = lax.axis_size("y")
    halves = n_y // (EXPERTS // lax.axis_size("req"))
    chunks = ROWS // CHUNK_ROWS
    pos = (flat_routes[:, None] * halves + jnp.arange(halves, dtype=jnp.int32)[None, :]) * CHUNK_ROWS
    pos = (pos + (slot_rank % CHUNK_ROWS)[:, None]).reshape(tok_rows, TOPK, halves)
    part_of = (slot_rank // CHUNK_ROWS).reshape(tok_rows, TOPK)
    row_ids = jnp.arange(EXPERTS * halves * CHUNK_ROWS, dtype=jnp.int32)
    placed = pos[:, :, :, None] == row_ids[None, None, None, :]
    swap = [(0, 1), (1, 0)]

    def expert_slice(rows):
        flat = rows.reshape(-1, model_width)
        gate = jnp.dot(flat, expert_gate[0], preferred_element_type=jnp.float32)
        up_val = jnp.dot(flat, expert_up[0], preferred_element_type=jnp.float32)
        hidden = ((up_val + 1.0) * gate * jax.nn.sigmoid(1.702 * gate)).astype(jnp.bfloat16)
        return jnp.dot(hidden, expert_down[0], preferred_element_type=jnp.float32).astype(
            jnp.bfloat16
        )

    tables, combines, received = [], [], []
    for part in range(chunks):
        match = placed & (part_of == part)[:, :, None, None]
        dispatch_table = jnp.any(match, axis=(1, 2)).T.astype(jnp.bfloat16)
        send_rows = jnp.dot(dispatch_table, normed2, preferred_element_type=jnp.float32).astype(
            jnp.bfloat16
        ).reshape(EXPERTS * halves, CHUNK_ROWS, model_width)
        combines.append(jnp.sum(jnp.where(match, weights[:, :, None, None], 0.0), axis=(1, 2)))
        received.append(
            lax.all_to_all(send_rows, ("req", "y"), split_axis=0, concat_axis=0, tiled=True)
        )
    chip_sums, returned = [], []
    for part in range(chunks):
        rows = received[part]
        if part > 0:
            rows, chip_sums[-1] = lax.optimization_barrier((rows, chip_sums[-1]))
            returned.append(
                lax.all_to_all(chip_sums[-1], ("req", "y"), split_axis=0, concat_axis=0, tiled=True)
            )
        sibling_rows = lax.ppermute(rows, "c", perm=swap)
        own_out = expert_slice(rows)
        sibling_out = expert_slice(sibling_rows)
        from_sibling = lax.ppermute(sibling_out, "c", perm=swap)
        chip_sum = (own_out.astype(jnp.float32) + from_sibling.astype(jnp.float32)).astype(
            jnp.bfloat16
        )
        chip_sums.append(chip_sum.reshape(rows.shape))
        if part > 0:
            returned[-1], chip_sums[-1] = lax.optimization_barrier((returned[-1], chip_sums[-1]))
    returned.append(
        lax.all_to_all(chip_sums[-1], ("req", "y"), split_axis=0, concat_axis=0, tiled=True)
    )
    moe_sum = jnp.zeros((tok_rows, model_width), jnp.float32)
    for combine, back in zip(combines, returned):
        back = back.reshape(-1, model_width)
        combine_hi = combine.astype(jnp.bfloat16)
        combine_lo = (combine - combine_hi.astype(jnp.float32)).astype(jnp.bfloat16)
        moe_sum = moe_sum + jnp.dot(combine_hi, back, preferred_element_type=jnp.float32)
        moe_sum = moe_sum + jnp.dot(combine_lo, back, preferred_element_type=jnp.float32)
    return (residual.astype(jnp.float32) + moe_sum).astype(jnp.bfloat16)


def solution(mesh):
    n_req, n_exp = mesh.devices.shape
    fine = jax.sharding.Mesh(mesh.devices.reshape(n_req, n_exp // 2, 2), ("req", "y", "c"))
    tok = ("req", "y", "c")
    return jax.shard_map(
        per_device,
        mesh=fine,
        in_specs=(
            P(tok, None),
            P(),
            P(None, ("y", "c")),
            P(None, ("y", "c")),
            P(None, ("y", "c")),
            P(("y", "c")),
            P(("y", "c"), None),
            P(),
            P(),
            P(tok, None),
            P("req", None),
            P(tok, None, None),
            P(tok, None, None),
            P(tok, None, None),
        ),
        out_specs=P(tok, None),
        check_vma=False,
    )
```

```python
import jax
import jax.numpy as jnp
from jax import lax
from jax.sharding import PartitionSpec as P

QUERY_HEADS = 64
KEY_VALUE_HEADS = 8
HEAD_DIM = 64
EXPERTS = 32
TOPK = 4
CAP = 14
ROWS = 16
CHUNK_ROWS = 8
LONGEST = 384
QUERY_BLOCKS = 4


def rms_norm(value_rows, gain):
    mean_sq = jnp.mean(value_rows * value_rows, axis=-1, keepdims=True)
    return value_rows * lax.rsqrt(mean_sq + 1e-05) * gain


def rotate(value_rows, offset):
    half = value_rows.shape[-1] // 2
    freqs = jnp.exp(
        -(2.0 * jnp.arange(half, dtype=jnp.float32) / value_rows.shape[-1])
        * jnp.log(jnp.float32(150000.0))
    )
    angle = offset.astype(jnp.float32)[:, None] * freqs[None, :]
    cosine = jnp.cos(angle)[:, None, :]
    sine = jnp.sin(angle)[:, None, :]
    first = value_rows[..., :half]
    second = value_rows[..., half:]
    return jnp.concatenate(
        [first * cosine - second * sine, second * cosine + first * sine], axis=-1
    )


def per_device(
    tokens,
    attn_gain,
    w_query,
    key_weight,
    value_weight,
    sinks,
    w_out,
    ffn_gain,
    router,
    routes,
    lengths,
    expert_gate,
    expert_up,
    expert_down,
):
    tok_rows = tokens.shape[0]
    model_width = tokens.shape[1]
    local_heads = w_query.shape[1] // HEAD_DIM
    local_kv = key_weight.shape[1] // HEAD_DIM
    head_group = QUERY_HEADS // KEY_VALUE_HEADS
    normed_input = rms_norm(tokens.astype(jnp.float32), attn_gain).astype(jnp.bfloat16)
    piece = lax.all_gather(normed_input, ("y", "c"), axis=0, tiled=True)
    projected = jnp.concatenate(
        [
            jnp.dot(piece, w_query, preferred_element_type=jnp.float32),
            jnp.dot(piece, key_weight, preferred_element_type=jnp.float32),
            jnp.dot(piece, value_weight, preferred_element_type=jnp.float32),
        ],
        axis=1,
    )
    item_count = projected.shape[0]
    lens = lengths[0]
    ends = jnp.cumsum(lens)
    starts = ends - lens
    position = jnp.arange(item_count, dtype=jnp.int32)
    member = ((position[:, None] >= starts[None, :]) & (position[:, None] < ends[None, :])).astype(
        jnp.int32
    )
    segment = jnp.sum(member * jnp.arange(lens.shape[0], dtype=jnp.int32)[None, :], axis=1)
    offset = position - jnp.sum(member * starts[None, :], axis=1)
    q_width = local_heads * HEAD_DIM
    kv_width = local_kv * HEAD_DIM
    query_rows = rotate(
        projected[:, :q_width].reshape(item_count, local_heads, HEAD_DIM), offset
    ).astype(jnp.bfloat16)
    key_rows = rotate(
        projected[:, q_width : q_width + kv_width].reshape(item_count, local_kv, HEAD_DIM), offset
    ).astype(jnp.bfloat16)
    value_rows = (
        projected[:, q_width + kv_width :]
        .reshape(item_count, local_kv, HEAD_DIM)
        .astype(jnp.bfloat16)
    )
    grouped_heads = query_rows.reshape(item_count, local_kv, head_group, HEAD_DIM)
    sink_score_logit = sinks.reshape(local_kv, head_group, 1, 1)
    block = item_count // QUERY_BLOCKS
    pieces = []
    for b in range(QUERY_BLOCKS):
        q0, q1 = b * block, (b + 1) * block
        k0 = max(0, (q0 - LONGEST + 1) // block * block)
        scores = jnp.einsum(
            "qcgd,kcd->cgqk", grouped_heads[q0:q1], key_rows[k0:q1], preferred_element_type=jnp.float32
        ) * HEAD_DIM ** (-0.5)
        allowed = (segment[q0:q1, None] == segment[None, k0:q1]) & (
            position[None, k0:q1] <= position[q0:q1, None]
        )
        masked = jnp.where(allowed[None, None], scores, -jnp.inf)
        top = jnp.maximum(jnp.max(masked, axis=-1, keepdims=True), sink_score_logit)
        expo = jnp.where(allowed[None, None], jnp.exp(scores - top), 0.0)
        denom = jnp.sum(expo, axis=-1, keepdims=True) + jnp.exp(sink_score_logit - top)
        probs = (expo / denom).astype(jnp.bfloat16)
        pieces.append(
            jnp.einsum("cgqk,kcd->qcgd", probs, value_rows[k0:q1], preferred_element_type=jnp.float32)
        )
    attended = jnp.concatenate(pieces, axis=0)
    attended = attended.reshape(item_count, q_width).astype(jnp.bfloat16)
    attn_sum = lax.psum_scatter(
        jnp.dot(attended, w_out, preferred_element_type=jnp.float32).astype(jnp.bfloat16),
        ("y", "c"),
        scatter_dimension=0,
        tiled=True,
    ).astype(jnp.float32)
    residual = (tokens.astype(jnp.float32) + attn_sum).astype(jnp.bfloat16)
    normed2 = rms_norm(residual.astype(jnp.float32), ffn_gain).astype(jnp.bfloat16)
    logits = jnp.dot(normed2, router, preferred_element_type=jnp.float32)
    picked = jnp.take_along_axis(logits, routes, axis=1)
    weights = jax.nn.softmax(picked, axis=-1)
    flat_routes = routes.reshape(-1)
    expert_ids = jnp.arange(EXPERTS, dtype=jnp.int32)
    onehot_route = (flat_routes[:, None] == expert_ids[None, :]).astype(jnp.int32)
    rank = jnp.cumsum(onehot_route, axis=0) - 1
    slot_rank = jnp.sum(onehot_route * rank, axis=1)
    n_y = lax.axis_size("y")
    halves = n_y // (EXPERTS // lax.axis_size("req"))
    chunks = ROWS // CHUNK_ROWS
    pos = (flat_routes[:, None] * halves + jnp.arange(halves, dtype=jnp.int32)[None, :]) * CHUNK_ROWS
    pos = (pos + (slot_rank % CHUNK_ROWS)[:, None]).reshape(tok_rows, TOPK, halves)
    part_of = (slot_rank // CHUNK_ROWS).reshape(tok_rows, TOPK)
    row_ids = jnp.arange(EXPERTS * halves * CHUNK_ROWS, dtype=jnp.int32)
    placed = pos[:, :, :, None] == row_ids[None, None, None, :]
    swap = [(0, 1), (1, 0)]

    def expert_slice(rows):
        flat = rows.reshape(-1, model_width)
        gate = jnp.dot(flat, expert_gate[0], preferred_element_type=jnp.float32)
        up_val = jnp.dot(flat, expert_up[0], preferred_element_type=jnp.float32)
        hidden = ((up_val + 1.0) * gate * jax.nn.sigmoid(1.702 * gate)).astype(jnp.bfloat16)
        return jnp.dot(hidden, expert_down[0], preferred_element_type=jnp.float32).astype(
            jnp.bfloat16
        )

    tables, combines, received = [], [], []
    for part in range(chunks):
        match = placed & (part_of == part)[:, :, None, None]
        dispatch_table = jnp.any(match, axis=(1, 2)).T.astype(jnp.bfloat16)
        send_rows = jnp.dot(dispatch_table, normed2, preferred_element_type=jnp.float32).astype(
            jnp.bfloat16
        ).reshape(EXPERTS * halves, CHUNK_ROWS, model_width)
        combines.append(jnp.sum(jnp.where(match, weights[:, :, None, None], 0.0), axis=(1, 2)))
        received.append(
            lax.all_to_all(send_rows, ("req", "y"), split_axis=0, concat_axis=0, tiled=True)
        )
    chip_sums, returned = [], []
    for part in range(chunks):
        rows = received[part]
        if part > 0:
            rows, chip_sums[-1] = lax.optimization_barrier((rows, chip_sums[-1]))
            returned.append(
                lax.all_to_all(chip_sums[-1], ("req", "y"), split_axis=0, concat_axis=0, tiled=True)
            )
        sibling_rows = lax.ppermute(rows, "c", perm=swap)
        own_out = expert_slice(rows)
        sibling_out = expert_slice(sibling_rows)
        from_sibling = lax.ppermute(sibling_out, "c", perm=swap)
        chip_sum = (own_out.astype(jnp.float32) + from_sibling.astype(jnp.float32)).astype(
            jnp.bfloat16
        )
        chip_sums.append(chip_sum.reshape(rows.shape))
        if part > 0:
            returned[-1], chip_sums[-1] = lax.optimization_barrier((returned[-1], chip_sums[-1]))
    returned.append(
        lax.all_to_all(chip_sums[-1], ("req", "y"), split_axis=0, concat_axis=0, tiled=True)
    )
    moe_sum = jnp.zeros((tok_rows, model_width), jnp.float32)
    for combine, back in zip(combines, returned):
        back = back.reshape(-1, model_width)
        combine_hi = combine.astype(jnp.bfloat16)
        combine_lo = (combine - combine_hi.astype(jnp.float32)).astype(jnp.bfloat16)
        moe_sum = moe_sum + jnp.dot(combine_hi, back, preferred_element_type=jnp.float32)
        moe_sum = moe_sum + jnp.dot(combine_lo, back, preferred_element_type=jnp.float32)
    return (residual.astype(jnp.float32) + moe_sum).astype(jnp.bfloat16)


def solution(mesh):
    n_req, n_exp = mesh.devices.shape
    fine = jax.sharding.Mesh(mesh.devices.reshape(n_req, n_exp // 2, 2), ("req", "y", "c"))
    tok = ("req", "y", "c")
    return jax.shard_map(
        per_device,
        mesh=fine,
        in_specs=(
            P(tok, None),
            P(),
            P(None, ("y", "c")),
            P(None, ("y", "c")),
            P(None, ("y", "c")),
            P(("y", "c")),
            P(("y", "c"), None),
            P(),
            P(),
            P(tok, None),
            P("req", None),
            P(tok, None, None),
            P(tok, None, None),
            P(tok, None, None),
        ),
        out_specs=P(tok, None),
        check_vma=False,
    )
```

```python
import jax
import jax.numpy as jnp
from jax import lax
from jax.experimental.layout import Layout, with_layout_constraint
from jax.sharding import PartitionSpec as P

QUERY_HEADS = 64
KEY_VALUE_HEADS = 8
HEAD_DIM = 64
EXPERTS = 32
TOPK = 4
CAP = 14
ROWS = 16
CHUNK_ROWS = 8
LONGEST = 384
QUERY_BLOCKS = 4


def rms_norm(value_rows, gain):
    mean_sq = jnp.mean(value_rows * value_rows, axis=-1, keepdims=True)
    return value_rows * lax.rsqrt(mean_sq + 1e-05) * gain


def rotate(value_rows, offset):
    half = value_rows.shape[-1] // 2
    freqs = jnp.exp(
        -(2.0 * jnp.arange(half, dtype=jnp.float32) / value_rows.shape[-1])
        * jnp.log(jnp.float32(150000.0))
    )
    angle = offset.astype(jnp.float32)[:, None] * freqs[None, :]
    cosine = jnp.cos(angle)[:, None, :]
    sine = jnp.sin(angle)[:, None, :]
    first = value_rows[..., :half]
    second = value_rows[..., half:]
    return jnp.concatenate(
        [first * cosine - second * sine, second * cosine + first * sine], axis=-1
    )


def per_device(
    tokens,
    attn_gain,
    w_query,
    key_weight,
    value_weight,
    sinks,
    w_out,
    ffn_gain,
    router,
    routes,
    lengths,
    expert_gate,
    expert_up,
    expert_down,
):
    tok_rows = tokens.shape[0]
    model_width = tokens.shape[1]
    local_heads = w_query.shape[1] // HEAD_DIM
    local_kv = key_weight.shape[1] // HEAD_DIM
    head_group = QUERY_HEADS // KEY_VALUE_HEADS
    normed_input = rms_norm(tokens.astype(jnp.float32), attn_gain).astype(jnp.bfloat16)
    piece = lax.all_gather(normed_input, ("y", "c"), axis=0, tiled=True)
    projected = jnp.concatenate(
        [
            jnp.dot(piece, w_query, preferred_element_type=jnp.float32),
            jnp.dot(piece, key_weight, preferred_element_type=jnp.float32),
            jnp.dot(piece, value_weight, preferred_element_type=jnp.float32),
        ],
        axis=1,
    )
    item_count = projected.shape[0]
    lens = lengths[0]
    ends = jnp.cumsum(lens)
    starts = ends - lens
    position = jnp.arange(item_count, dtype=jnp.int32)
    member = ((position[:, None] >= starts[None, :]) & (position[:, None] < ends[None, :])).astype(
        jnp.int32
    )
    segment = jnp.sum(member * jnp.arange(lens.shape[0], dtype=jnp.int32)[None, :], axis=1)
    offset = position - jnp.sum(member * starts[None, :], axis=1)
    q_width = local_heads * HEAD_DIM
    kv_width = local_kv * HEAD_DIM
    query_rows = rotate(
        projected[:, :q_width].reshape(item_count, local_heads, HEAD_DIM), offset
    ).astype(jnp.bfloat16)
    key_rows = rotate(
        projected[:, q_width : q_width + kv_width].reshape(item_count, local_kv, HEAD_DIM), offset
    ).astype(jnp.bfloat16)
    value_rows = (
        projected[:, q_width + kv_width :]
        .reshape(item_count, local_kv, HEAD_DIM)
        .astype(jnp.bfloat16)
    )
    grouped_heads = query_rows.reshape(item_count, local_kv, head_group, HEAD_DIM)
    sink_score_logit = sinks.reshape(local_kv, head_group, 1, 1)
    block = item_count // QUERY_BLOCKS
    pieces = []
    for b in range(QUERY_BLOCKS):
        q0, q1 = b * block, (b + 1) * block
        k0 = max(0, (q0 - LONGEST + 1) // block * block)
        scores = jnp.einsum(
            "qcgd,kcd->cgqk", grouped_heads[q0:q1], key_rows[k0:q1], preferred_element_type=jnp.float32
        ) * HEAD_DIM ** (-0.5)
        allowed = (segment[q0:q1, None] == segment[None, k0:q1]) & (
            position[None, k0:q1] <= position[q0:q1, None]
        )
        masked = jnp.where(allowed[None, None], scores, -jnp.inf)
        top = jnp.maximum(jnp.max(masked, axis=-1, keepdims=True), sink_score_logit)
        expo = jnp.where(allowed[None, None], jnp.exp(scores - top), 0.0)
        denom = jnp.sum(expo, axis=-1, keepdims=True) + jnp.exp(sink_score_logit - top)
        probs = (expo / denom).astype(jnp.bfloat16)
        pieces.append(
            jnp.einsum("cgqk,kcd->qcgd", probs, value_rows[k0:q1], preferred_element_type=jnp.float32)
        )
    attended = jnp.concatenate(pieces, axis=0)
    attended = attended.reshape(item_count, q_width).astype(jnp.bfloat16)
    attn_sum = lax.psum_scatter(
        jnp.dot(attended, w_out, preferred_element_type=jnp.float32).astype(jnp.bfloat16),
        ("y", "c"),
        scatter_dimension=0,
        tiled=True,
    ).astype(jnp.float32)
    residual = (tokens.astype(jnp.float32) + attn_sum).astype(jnp.bfloat16)
    normed2 = rms_norm(residual.astype(jnp.float32), ffn_gain).astype(jnp.bfloat16)
    logits = jnp.dot(normed2, router, preferred_element_type=jnp.float32)
    picked = jnp.take_along_axis(logits, routes, axis=1)
    weights = jax.nn.softmax(picked, axis=-1)
    flat_routes = routes.reshape(-1)
    expert_ids = jnp.arange(EXPERTS, dtype=jnp.int32)
    onehot_route = (flat_routes[:, None] == expert_ids[None, :]).astype(jnp.int32)
    rank = jnp.cumsum(onehot_route, axis=0) - 1
    slot_rank = jnp.sum(onehot_route * rank, axis=1)
    n_y = lax.axis_size("y")
    halves = n_y // (EXPERTS // lax.axis_size("req"))
    chunks = ROWS // CHUNK_ROWS
    pos = (flat_routes[:, None] * halves + jnp.arange(halves, dtype=jnp.int32)[None, :]) * CHUNK_ROWS
    pos = (pos + (slot_rank % CHUNK_ROWS)[:, None]).reshape(tok_rows, TOPK, halves)
    part_of = (slot_rank // CHUNK_ROWS).reshape(tok_rows, TOPK)
    row_ids = jnp.arange(EXPERTS * halves * CHUNK_ROWS, dtype=jnp.int32)
    placed = pos[:, :, :, None] == row_ids[None, None, None, :]
    swap = [(0, 1), (1, 0)]

    def expert_slice(rows):
        flat = rows.reshape(-1, model_width)
        gate = jnp.dot(flat, expert_gate[0], preferred_element_type=jnp.float32)
        up_val = jnp.dot(flat, expert_up[0], preferred_element_type=jnp.float32)
        hidden = ((up_val + 1.0) * gate * jax.nn.sigmoid(1.702 * gate)).astype(jnp.bfloat16)
        return jnp.dot(hidden, expert_down[0], preferred_element_type=jnp.float32).astype(
            jnp.bfloat16
        )

    tables, combines, received = [], [], []
    for part in range(chunks):
        match = placed & (part_of == part)[:, :, None, None]
        dispatch_table = jnp.any(match, axis=(1, 2)).T.astype(jnp.bfloat16)
        send_rows = jnp.dot(dispatch_table, normed2, preferred_element_type=jnp.float32).astype(
            jnp.bfloat16
        )
        send_rows = with_layout_constraint(send_rows, Layout(major_to_minor=(0, 1))).reshape(
            EXPERTS * halves, CHUNK_ROWS, model_width
        )
        combines.append(jnp.sum(jnp.where(match, weights[:, :, None, None], 0.0), axis=(1, 2)))
        received.append(
            lax.all_to_all(send_rows, ("req", "y"), split_axis=0, concat_axis=0, tiled=True)
        )
    chip_sums, returned = [], []
    for part in range(chunks):
        rows = received[part]
        if part > 0:
            rows, chip_sums[-1] = lax.optimization_barrier((rows, chip_sums[-1]))
            returned.append(
                lax.all_to_all(chip_sums[-1], ("req", "y"), split_axis=0, concat_axis=0, tiled=True)
            )
        sibling_rows = lax.ppermute(rows, "c", perm=swap)
        own_out = expert_slice(rows)
        sibling_out = expert_slice(sibling_rows)
        from_sibling = lax.ppermute(sibling_out, "c", perm=swap)
        chip_sum = (own_out.astype(jnp.float32) + from_sibling.astype(jnp.float32)).astype(
            jnp.bfloat16
        )
        chip_sum = with_layout_constraint(chip_sum, Layout(major_to_minor=(0, 1)))
        chip_sums.append(chip_sum.reshape(rows.shape))
        if part > 0:
            returned[-1], chip_sums[-1] = lax.optimization_barrier((returned[-1], chip_sums[-1]))
    returned.append(
        lax.all_to_all(chip_sums[-1], ("req", "y"), split_axis=0, concat_axis=0, tiled=True)
    )
    moe_sum = jnp.zeros((tok_rows, model_width), jnp.float32)
    for combine, back in zip(combines, returned):
        back = back.reshape(-1, model_width)
        combine_hi = combine.astype(jnp.bfloat16)
        combine_lo = (combine - combine_hi.astype(jnp.float32)).astype(jnp.bfloat16)
        moe_sum = moe_sum + jnp.dot(combine_hi, back, preferred_element_type=jnp.float32)
        moe_sum = moe_sum + jnp.dot(combine_lo, back, preferred_element_type=jnp.float32)
    return (residual.astype(jnp.float32) + moe_sum).astype(jnp.bfloat16)


def solution(mesh):
    n_req, n_exp = mesh.devices.shape
    fine = jax.sharding.Mesh(mesh.devices.reshape(n_req, n_exp // 2, 2), ("req", "y", "c"))
    tok = ("req", "y", "c")
    return jax.shard_map(
        per_device,
        mesh=fine,
        in_specs=(
            P(tok, None),
            P(),
            P(None, ("y", "c")),
            P(None, ("y", "c")),
            P(None, ("y", "c")),
            P(("y", "c")),
            P(("y", "c"), None),
            P(),
            P(),
            P(tok, None),
            P("req", None),
            P(tok, None, None),
            P(tok, None, None),
            P(tok, None, None),
        ),
        out_specs=P(tok, None),
        check_vma=False,
    )
```

```python
import jax
import jax.numpy as jnp
from jax import lax
from jax.experimental.layout import Layout, with_layout_constraint
from jax.sharding import PartitionSpec as P

QUERY_HEADS = 64
KEY_VALUE_HEADS = 8
HEAD_DIM = 64
EXPERTS = 32
TOPK = 4
CAP = 14
ROWS = 16
CHUNK_ROWS = 8
LONGEST = 384
QUERY_BLOCKS = 8


def rms_norm(value_rows, gain):
    mean_sq = jnp.mean(value_rows * value_rows, axis=-1, keepdims=True)
    return value_rows * lax.rsqrt(mean_sq + 1e-05) * gain


def rotate(value_rows, offset):
    half = value_rows.shape[-1] // 2
    freqs = jnp.exp(
        -(2.0 * jnp.arange(half, dtype=jnp.float32) / value_rows.shape[-1])
        * jnp.log(jnp.float32(150000.0))
    )
    angle = offset.astype(jnp.float32)[:, None] * freqs[None, :]
    cosine = jnp.cos(angle)[:, None, :]
    sine = jnp.sin(angle)[:, None, :]
    first = value_rows[..., :half]
    second = value_rows[..., half:]
    return jnp.concatenate(
        [first * cosine - second * sine, second * cosine + first * sine], axis=-1
    )


def per_device(
    tokens,
    attn_gain,
    w_query,
    key_weight,
    value_weight,
    sinks,
    w_out,
    ffn_gain,
    router,
    routes,
    lengths,
    expert_gate,
    expert_up,
    expert_down,
):
    tok_rows = tokens.shape[0]
    model_width = tokens.shape[1]
    local_heads = w_query.shape[1] // HEAD_DIM
    local_kv = key_weight.shape[1] // HEAD_DIM
    head_group = QUERY_HEADS // KEY_VALUE_HEADS
    normed_input = rms_norm(tokens.astype(jnp.float32), attn_gain).astype(jnp.bfloat16)
    piece = lax.all_gather(normed_input, ("y", "c"), axis=0, tiled=True)
    projected = jnp.concatenate(
        [
            jnp.dot(piece, w_query, preferred_element_type=jnp.float32),
            jnp.dot(piece, key_weight, preferred_element_type=jnp.float32),
            jnp.dot(piece, value_weight, preferred_element_type=jnp.float32),
        ],
        axis=1,
    )
    item_count = projected.shape[0]
    lens = lengths[0]
    ends = jnp.cumsum(lens)
    starts = ends - lens
    position = jnp.arange(item_count, dtype=jnp.int32)
    member = ((position[:, None] >= starts[None, :]) & (position[:, None] < ends[None, :])).astype(
        jnp.int32
    )
    segment = jnp.sum(member * jnp.arange(lens.shape[0], dtype=jnp.int32)[None, :], axis=1)
    offset = position - jnp.sum(member * starts[None, :], axis=1)
    q_width = local_heads * HEAD_DIM
    kv_width = local_kv * HEAD_DIM
    query_rows = rotate(
        projected[:, :q_width].reshape(item_count, local_heads, HEAD_DIM), offset
    ).astype(jnp.bfloat16)
    key_rows = rotate(
        projected[:, q_width : q_width + kv_width].reshape(item_count, local_kv, HEAD_DIM), offset
    ).astype(jnp.bfloat16)
    value_rows = (
        projected[:, q_width + kv_width :]
        .reshape(item_count, local_kv, HEAD_DIM)
        .astype(jnp.bfloat16)
    )
    grouped_heads = query_rows.reshape(item_count, local_kv, head_group, HEAD_DIM)
    sink_score_logit = sinks.reshape(local_kv, head_group, 1, 1)
    block = item_count // QUERY_BLOCKS
    pieces = []
    for b in range(QUERY_BLOCKS):
        q0, q1 = b * block, (b + 1) * block
        k0 = max(0, (q0 - LONGEST + 1) // block * block)
        scores = jnp.einsum(
            "qcgd,kcd->cgqk", grouped_heads[q0:q1], key_rows[k0:q1], preferred_element_type=jnp.float32
        ) * HEAD_DIM ** (-0.5)
        allowed = (segment[q0:q1, None] == segment[None, k0:q1]) & (
            position[None, k0:q1] <= position[q0:q1, None]
        )
        masked = jnp.where(allowed[None, None], scores, -jnp.inf)
        top = jnp.maximum(jnp.max(masked, axis=-1, keepdims=True), sink_score_logit)
        expo = jnp.where(allowed[None, None], jnp.exp(scores - top), 0.0)
        denom = jnp.sum(expo, axis=-1, keepdims=True) + jnp.exp(sink_score_logit - top)
        probs = (expo / denom).astype(jnp.bfloat16)
        pieces.append(
            jnp.einsum("cgqk,kcd->qcgd", probs, value_rows[k0:q1], preferred_element_type=jnp.float32)
        )
    attended = jnp.concatenate(pieces, axis=0)
    attended = attended.reshape(item_count, q_width).astype(jnp.bfloat16)
    attn_sum = lax.psum_scatter(
        jnp.dot(attended, w_out, preferred_element_type=jnp.float32).astype(jnp.bfloat16),
        ("y", "c"),
        scatter_dimension=0,
        tiled=True,
    ).astype(jnp.float32)
    residual = (tokens.astype(jnp.float32) + attn_sum).astype(jnp.bfloat16)
    normed2 = rms_norm(residual.astype(jnp.float32), ffn_gain).astype(jnp.bfloat16)
    logits = jnp.dot(normed2, router, preferred_element_type=jnp.float32)
    picked = jnp.take_along_axis(logits, routes, axis=1)
    weights = jax.nn.softmax(picked, axis=-1)
    flat_routes = routes.reshape(-1)
    expert_ids = jnp.arange(EXPERTS, dtype=jnp.int32)
    onehot_route = (flat_routes[:, None] == expert_ids[None, :]).astype(jnp.int32)
    rank = jnp.cumsum(onehot_route, axis=0) - 1
    slot_rank = jnp.sum(onehot_route * rank, axis=1)
    n_y = lax.axis_size("y")
    halves = n_y // (EXPERTS // lax.axis_size("req"))
    chunks = ROWS // CHUNK_ROWS
    pos = (flat_routes[:, None] * halves + jnp.arange(halves, dtype=jnp.int32)[None, :]) * CHUNK_ROWS
    pos = (pos + (slot_rank % CHUNK_ROWS)[:, None]).reshape(tok_rows, TOPK, halves)
    part_of = (slot_rank // CHUNK_ROWS).reshape(tok_rows, TOPK)
    row_ids = jnp.arange(EXPERTS * halves * CHUNK_ROWS, dtype=jnp.int32)
    placed = pos[:, :, :, None] == row_ids[None, None, None, :]
    swap = [(0, 1), (1, 0)]

    def expert_slice(rows):
        flat = rows.reshape(-1, model_width)
        gate = jnp.dot(flat, expert_gate[0], preferred_element_type=jnp.float32)
        up_val = jnp.dot(flat, expert_up[0], preferred_element_type=jnp.float32)
        hidden = ((up_val + 1.0) * gate * jax.nn.sigmoid(1.702 * gate)).astype(jnp.bfloat16)
        return jnp.dot(hidden, expert_down[0], preferred_element_type=jnp.float32).astype(
            jnp.bfloat16
        )

    tables, combines, received = [], [], []
    for part in range(chunks):
        match = placed & (part_of == part)[:, :, None, None]
        dispatch_table = jnp.any(match, axis=(1, 2)).T.astype(jnp.bfloat16)
        send_rows = jnp.dot(dispatch_table, normed2, preferred_element_type=jnp.float32).astype(
            jnp.bfloat16
        )
        send_rows = with_layout_constraint(send_rows, Layout(major_to_minor=(0, 1))).reshape(
            EXPERTS * halves, CHUNK_ROWS, model_width
        )
        combines.append(jnp.sum(jnp.where(match, weights[:, :, None, None], 0.0), axis=(1, 2)))
        received.append(
            lax.all_to_all(send_rows, ("req", "y"), split_axis=0, concat_axis=0, tiled=True)
        )
    chip_sums, returned = [], []
    for part in range(chunks):
        rows = received[part]
        if part > 0:
            rows, chip_sums[-1] = lax.optimization_barrier((rows, chip_sums[-1]))
            returned.append(
                lax.all_to_all(chip_sums[-1], ("req", "y"), split_axis=0, concat_axis=0, tiled=True)
            )
        sibling_rows = lax.ppermute(rows, "c", perm=swap)
        own_out = expert_slice(rows)
        sibling_out = expert_slice(sibling_rows)
        from_sibling = lax.ppermute(sibling_out, "c", perm=swap)
        chip_sum = (own_out.astype(jnp.float32) + from_sibling.astype(jnp.float32)).astype(
            jnp.bfloat16
        )
        chip_sum = with_layout_constraint(chip_sum, Layout(major_to_minor=(0, 1)))
        chip_sums.append(chip_sum.reshape(rows.shape))
        if part > 0:
            returned[-1], chip_sums[-1] = lax.optimization_barrier((returned[-1], chip_sums[-1]))
    returned.append(
        lax.all_to_all(chip_sums[-1], ("req", "y"), split_axis=0, concat_axis=0, tiled=True)
    )
    moe_sum = jnp.zeros((tok_rows, model_width), jnp.float32)
    for combine, back in zip(combines, returned):
        back = back.reshape(-1, model_width)
        combine_hi = combine.astype(jnp.bfloat16)
        combine_lo = (combine - combine_hi.astype(jnp.float32)).astype(jnp.bfloat16)
        moe_sum = moe_sum + jnp.dot(combine_hi, back, preferred_element_type=jnp.float32)
        moe_sum = moe_sum + jnp.dot(combine_lo, back, preferred_element_type=jnp.float32)
    return (residual.astype(jnp.float32) + moe_sum).astype(jnp.bfloat16)


def solution(mesh):
    n_req, n_exp = mesh.devices.shape
    fine = jax.sharding.Mesh(mesh.devices.reshape(n_req, n_exp // 2, 2), ("req", "y", "c"))
    tok = ("req", "y", "c")
    return jax.shard_map(
        per_device,
        mesh=fine,
        in_specs=(
            P(tok, None),
            P(),
            P(None, ("y", "c")),
            P(None, ("y", "c")),
            P(None, ("y", "c")),
            P(("y", "c")),
            P(("y", "c"), None),
            P(),
            P(),
            P(tok, None),
            P("req", None),
            P(tok, None, None),
            P(tok, None, None),
            P(tok, None, None),
        ),
        out_specs=P(tok, None),
        check_vma=False,
    )
```

```python
import jax
import jax.numpy as jnp
from jax import lax
from jax.experimental.layout import Layout, with_layout_constraint
from jax.sharding import PartitionSpec as P

QUERY_HEADS = 64
KEY_VALUE_HEADS = 8
HEAD_DIM = 64
EXPERTS = 32
TOPK = 4
CAP = 14
ROWS = 16
CHUNK_ROWS = 8
LONGEST = 384
QUERY_BLOCKS = 4


def rms_norm(value_rows, gain):
    mean_sq = jnp.mean(value_rows * value_rows, axis=-1, keepdims=True)
    return value_rows * lax.rsqrt(mean_sq + 1e-05) * gain


def rotate(value_rows, offset):
    half = value_rows.shape[-1] // 2
    freqs = jnp.exp(
        -(2.0 * jnp.arange(half, dtype=jnp.float32) / value_rows.shape[-1])
        * jnp.log(jnp.float32(150000.0))
    )
    angle = offset.astype(jnp.float32)[:, None] * freqs[None, :]
    cosine = jnp.cos(angle)[:, None, :]
    sine = jnp.sin(angle)[:, None, :]
    first = value_rows[..., :half]
    second = value_rows[..., half:]
    return jnp.concatenate(
        [first * cosine - second * sine, second * cosine + first * sine], axis=-1
    )


def per_device(
    tokens,
    attn_gain,
    w_query,
    key_weight,
    value_weight,
    sinks,
    w_out,
    ffn_gain,
    router,
    routes,
    lengths,
    expert_gate,
    expert_up,
    expert_down,
):
    tok_rows = tokens.shape[0]
    model_width = tokens.shape[1]
    local_heads = w_query.shape[1] // HEAD_DIM
    local_kv = key_weight.shape[1] // HEAD_DIM
    head_group = QUERY_HEADS // KEY_VALUE_HEADS
    normed_input = rms_norm(tokens.astype(jnp.float32), attn_gain).astype(jnp.bfloat16)
    piece = lax.all_gather(normed_input, ("y", "c"), axis=0, tiled=True)
    projected = jnp.concatenate(
        [
            jnp.dot(piece, w_query, preferred_element_type=jnp.float32),
            jnp.dot(piece, key_weight, preferred_element_type=jnp.float32),
            jnp.dot(piece, value_weight, preferred_element_type=jnp.float32),
        ],
        axis=1,
    )
    item_count = projected.shape[0]
    lens = lengths[0]
    ends = jnp.cumsum(lens)
    starts = ends - lens
    position = jnp.arange(item_count, dtype=jnp.int32)
    member = ((position[:, None] >= starts[None, :]) & (position[:, None] < ends[None, :])).astype(
        jnp.int32
    )
    segment = jnp.sum(member * jnp.arange(lens.shape[0], dtype=jnp.int32)[None, :], axis=1)
    offset = position - jnp.sum(member * starts[None, :], axis=1)
    q_width = local_heads * HEAD_DIM
    kv_width = local_kv * HEAD_DIM
    query_rows = rotate(
        projected[:, :q_width].reshape(item_count, local_heads, HEAD_DIM), offset
    ).astype(jnp.bfloat16)
    key_rows = rotate(
        projected[:, q_width : q_width + kv_width].reshape(item_count, local_kv, HEAD_DIM), offset
    ).astype(jnp.bfloat16)
    value_rows = (
        projected[:, q_width + kv_width :]
        .reshape(item_count, local_kv, HEAD_DIM)
        .astype(jnp.bfloat16)
    )
    grouped_heads = query_rows.reshape(item_count, local_kv, head_group, HEAD_DIM)
    sink_score_logit = sinks.reshape(local_kv, head_group, 1, 1)
    block = item_count // QUERY_BLOCKS
    pieces = []
    for b in range(QUERY_BLOCKS):
        q0, q1 = b * block, (b + 1) * block
        k0 = max(0, (q0 - LONGEST + 1) // block * block)
        scores = jnp.einsum(
            "qcgd,kcd->cgqk", grouped_heads[q0:q1], key_rows[k0:q1], preferred_element_type=jnp.float32
        ) * HEAD_DIM ** (-0.5)
        allowed = (segment[q0:q1, None] == segment[None, k0:q1]) & (
            position[None, k0:q1] <= position[q0:q1, None]
        )
        masked = jnp.where(allowed[None, None], scores, -jnp.inf)
        top = jnp.maximum(jnp.max(masked, axis=-1, keepdims=True), sink_score_logit)
        expo = jnp.where(allowed[None, None], jnp.exp(scores - top), 0.0)
        denom = jnp.sum(expo, axis=-1, keepdims=True) + jnp.exp(sink_score_logit - top)
        probs = (expo / denom).astype(jnp.bfloat16)
        pieces.append(
            jnp.einsum("cgqk,kcd->qcgd", probs, value_rows[k0:q1], preferred_element_type=jnp.float32)
        )
    attended = jnp.concatenate(pieces, axis=0)
    attended = attended.reshape(item_count, q_width).astype(jnp.bfloat16)
    swap = [(0, 1), (1, 0)]
    sibling_weights = [lax.ppermute(w[0], "c", perm=swap) for w in (expert_gate, expert_up, expert_down)]
    attended, *sibling_weights = lax.optimization_barrier((attended, *sibling_weights))
    attn_sum = lax.psum_scatter(
        jnp.dot(attended, w_out, preferred_element_type=jnp.float32).astype(jnp.bfloat16),
        ("y", "c"),
        scatter_dimension=0,
        tiled=True,
    ).astype(jnp.float32)
    residual = (tokens.astype(jnp.float32) + attn_sum).astype(jnp.bfloat16)
    normed2 = rms_norm(residual.astype(jnp.float32), ffn_gain).astype(jnp.bfloat16)
    logits = jnp.dot(normed2, router, preferred_element_type=jnp.float32)
    picked = jnp.take_along_axis(logits, routes, axis=1)
    weights = jax.nn.softmax(picked, axis=-1)
    flat_routes = routes.reshape(-1)
    expert_ids = jnp.arange(EXPERTS, dtype=jnp.int32)
    onehot_route = (flat_routes[:, None] == expert_ids[None, :]).astype(jnp.int32)
    rank = jnp.cumsum(onehot_route, axis=0) - 1
    slot_rank = jnp.sum(onehot_route * rank, axis=1)
    n_y = lax.axis_size("y")
    halves = n_y // (EXPERTS // lax.axis_size("req"))
    chunks = ROWS // CHUNK_ROWS
    pos = (flat_routes[:, None] * halves + jnp.arange(halves, dtype=jnp.int32)[None, :]) * CHUNK_ROWS
    pos = (pos + (slot_rank % CHUNK_ROWS)[:, None]).reshape(tok_rows, TOPK, halves)
    part_of = (slot_rank // CHUNK_ROWS).reshape(tok_rows, TOPK)
    row_ids = jnp.arange(EXPERTS * halves * CHUNK_ROWS, dtype=jnp.int32)
    placed = pos[:, :, :, None] == row_ids[None, None, None, :]

    def expert_slice(rows, gate_w, up_w, down_w):
        flat = rows.reshape(-1, model_width)
        gate = jnp.dot(flat, gate_w, preferred_element_type=jnp.float32)
        up_val = jnp.dot(flat, up_w, preferred_element_type=jnp.float32)
        hidden = ((up_val + 1.0) * gate * jax.nn.sigmoid(1.702 * gate)).astype(jnp.bfloat16)
        return jnp.dot(hidden, down_w, preferred_element_type=jnp.float32).astype(jnp.bfloat16)

    tables, combines, received = [], [], []
    for part in range(chunks):
        match = placed & (part_of == part)[:, :, None, None]
        dispatch_table = jnp.any(match, axis=(1, 2)).T.astype(jnp.bfloat16)
        send_rows = jnp.dot(dispatch_table, normed2, preferred_element_type=jnp.float32).astype(
            jnp.bfloat16
        )
        send_rows = with_layout_constraint(send_rows, Layout(major_to_minor=(0, 1))).reshape(
            EXPERTS * halves, CHUNK_ROWS, model_width
        )
        combines.append(jnp.sum(jnp.where(match, weights[:, :, None, None], 0.0), axis=(1, 2)))
        received.append(
            lax.all_to_all(send_rows, ("req", "y"), split_axis=0, concat_axis=0, tiled=True)
        )
    chip_sums, returned = [], []
    for part in range(chunks):
        rows = received[part]
        if part > 0:
            rows, chip_sums[-1] = lax.optimization_barrier((rows, chip_sums[-1]))
            returned.append(
                lax.all_to_all(chip_sums[-1], ("req", "y"), split_axis=0, concat_axis=0, tiled=True)
            )
        own_out = expert_slice(rows, expert_gate[0], expert_up[0], expert_down[0])
        sibling_out = expert_slice(rows, *sibling_weights)
        chip_sum = (own_out.astype(jnp.float32) + sibling_out.astype(jnp.float32)).astype(
            jnp.bfloat16
        )
        chip_sum = with_layout_constraint(chip_sum, Layout(major_to_minor=(0, 1)))
        chip_sums.append(chip_sum.reshape(rows.shape))
        if part > 0:
            returned[-1], chip_sums[-1] = lax.optimization_barrier((returned[-1], chip_sums[-1]))
    returned.append(
        lax.all_to_all(chip_sums[-1], ("req", "y"), split_axis=0, concat_axis=0, tiled=True)
    )
    moe_sum = jnp.zeros((tok_rows, model_width), jnp.float32)
    for combine, back in zip(combines, returned):
        back = back.reshape(-1, model_width)
        combine_hi = combine.astype(jnp.bfloat16)
        combine_lo = (combine - combine_hi.astype(jnp.float32)).astype(jnp.bfloat16)
        moe_sum = moe_sum + jnp.dot(combine_hi, back, preferred_element_type=jnp.float32)
        moe_sum = moe_sum + jnp.dot(combine_lo, back, preferred_element_type=jnp.float32)
    return (residual.astype(jnp.float32) + moe_sum).astype(jnp.bfloat16)


def solution(mesh):
    n_req, n_exp = mesh.devices.shape
    fine = jax.sharding.Mesh(mesh.devices.reshape(n_req, n_exp // 2, 2), ("req", "y", "c"))
    tok = ("req", "y", "c")
    return jax.shard_map(
        per_device,
        mesh=fine,
        in_specs=(
            P(tok, None),
            P(),
            P(None, ("y", "c")),
            P(None, ("y", "c")),
            P(None, ("y", "c")),
            P(("y", "c")),
            P(("y", "c"), None),
            P(),
            P(),
            P(tok, None),
            P("req", None),
            P(tok, None, None),
            P(tok, None, None),
            P(tok, None, None),
        ),
        out_specs=P(tok, None),
        check_vma=False,
    )
```

```python
import jax
import jax.numpy as jnp
from jax import lax
from jax.experimental.layout import Layout, with_layout_constraint
from jax.sharding import PartitionSpec as P

QUERY_HEADS = 64
KEY_VALUE_HEADS = 8
HEAD_DIM = 64
EXPERTS = 32
TOPK = 4
CAP = 14
ROWS = 16
CHUNK_ROWS = 8
LONGEST = 384
QUERY_BLOCKS = 4


def rms_norm(value_rows, gain):
    mean_sq = jnp.mean(value_rows * value_rows, axis=-1, keepdims=True)
    return value_rows * lax.rsqrt(mean_sq + 1e-05) * gain


def rotate(value_rows, offset):
    half = value_rows.shape[-1] // 2
    freqs = jnp.exp(
        -(2.0 * jnp.arange(half, dtype=jnp.float32) / value_rows.shape[-1])
        * jnp.log(jnp.float32(150000.0))
    )
    angle = offset.astype(jnp.float32)[:, None] * freqs[None, :]
    cosine = jnp.cos(angle)[:, None, :]
    sine = jnp.sin(angle)[:, None, :]
    first = value_rows[..., :half]
    second = value_rows[..., half:]
    return jnp.concatenate(
        [first * cosine - second * sine, second * cosine + first * sine], axis=-1
    )


def per_device(
    tokens,
    attn_gain,
    w_query,
    key_weight,
    value_weight,
    sinks,
    w_out,
    ffn_gain,
    router,
    routes,
    lengths,
    expert_gate,
    expert_up,
    expert_down,
):
    tok_rows = tokens.shape[0]
    model_width = tokens.shape[1]
    local_heads = w_query.shape[1] // HEAD_DIM
    local_kv = key_weight.shape[1] // HEAD_DIM
    head_group = QUERY_HEADS // KEY_VALUE_HEADS
    normed_input = rms_norm(tokens.astype(jnp.float32), attn_gain).astype(jnp.bfloat16)
    piece = lax.all_gather(normed_input, ("y", "c"), axis=0, tiled=True)
    projected = jnp.concatenate(
        [
            jnp.dot(piece, w_query, preferred_element_type=jnp.float32),
            jnp.dot(piece, key_weight, preferred_element_type=jnp.float32),
            jnp.dot(piece, value_weight, preferred_element_type=jnp.float32),
        ],
        axis=1,
    )
    item_count = projected.shape[0]
    lens = lengths[0]
    ends = jnp.cumsum(lens)
    starts = ends - lens
    position = jnp.arange(item_count, dtype=jnp.int32)
    member = ((position[:, None] >= starts[None, :]) & (position[:, None] < ends[None, :])).astype(
        jnp.int32
    )
    segment = jnp.sum(member * jnp.arange(lens.shape[0], dtype=jnp.int32)[None, :], axis=1)
    offset = position - jnp.sum(member * starts[None, :], axis=1)
    q_width = local_heads * HEAD_DIM
    kv_width = local_kv * HEAD_DIM
    query_rows = rotate(
        projected[:, :q_width].reshape(item_count, local_heads, HEAD_DIM), offset
    ).astype(jnp.bfloat16)
    key_rows = rotate(
        projected[:, q_width : q_width + kv_width].reshape(item_count, local_kv, HEAD_DIM), offset
    ).astype(jnp.bfloat16)
    value_rows = (
        projected[:, q_width + kv_width :]
        .reshape(item_count, local_kv, HEAD_DIM)
        .astype(jnp.bfloat16)
    )
    grouped_heads = query_rows.reshape(item_count, local_kv, head_group, HEAD_DIM)
    sink_score_logit = sinks.reshape(local_kv, head_group, 1, 1)
    block = item_count // QUERY_BLOCKS
    pieces = []
    for b in range(QUERY_BLOCKS):
        q0, q1 = b * block, (b + 1) * block
        k0 = max(0, (q0 - LONGEST + 1) // block * block)
        scores = jnp.einsum(
            "qcgd,kcd->cgqk", grouped_heads[q0:q1], key_rows[k0:q1], preferred_element_type=jnp.float32
        ) * HEAD_DIM ** (-0.5)
        allowed = (segment[q0:q1, None] == segment[None, k0:q1]) & (
            position[None, k0:q1] <= position[q0:q1, None]
        )
        masked = jnp.where(allowed[None, None], scores, -jnp.inf)
        top = jnp.maximum(jnp.max(masked, axis=-1, keepdims=True), sink_score_logit)
        expo = jnp.where(allowed[None, None], jnp.exp(scores - top), 0.0)
        denom = jnp.sum(expo, axis=-1, keepdims=True) + jnp.exp(sink_score_logit - top)
        probs = (expo / denom).astype(jnp.bfloat16)
        pieces.append(
            jnp.einsum("cgqk,kcd->qcgd", probs, value_rows[k0:q1], preferred_element_type=jnp.float32)
        )
    attended = jnp.concatenate(pieces, axis=0)
    attended = attended.reshape(item_count, q_width).astype(jnp.bfloat16)
    swap = [(0, 1), (1, 0)]
    sibling_weights = [lax.ppermute(w[0], "c", perm=swap) for w in (expert_gate, expert_up, expert_down)]
    attended, *sibling_weights = lax.optimization_barrier((attended, *sibling_weights))
    attn_sum = lax.psum_scatter(
        jnp.dot(attended, w_out, preferred_element_type=jnp.float32).astype(jnp.bfloat16),
        ("y", "c"),
        scatter_dimension=0,
        tiled=True,
    ).astype(jnp.float32)
    residual = (tokens.astype(jnp.float32) + attn_sum).astype(jnp.bfloat16)
    normed2 = rms_norm(residual.astype(jnp.float32), ffn_gain).astype(jnp.bfloat16)
    logits = jnp.dot(normed2, router, preferred_element_type=jnp.float32)
    picked = jnp.take_along_axis(logits, routes, axis=1)
    weights = jax.nn.softmax(picked, axis=-1)
    flat_routes = routes.reshape(-1)
    expert_ids = jnp.arange(EXPERTS, dtype=jnp.int32)
    onehot_route = (flat_routes[:, None] == expert_ids[None, :]).astype(jnp.int32)
    rank = jnp.cumsum(onehot_route, axis=0) - 1
    slot_rank = jnp.sum(onehot_route * rank, axis=1)
    n_y = lax.axis_size("y")
    halves = n_y // (EXPERTS // lax.axis_size("req"))
    bounds = ((0, CHUNK_ROWS), (CHUNK_ROWS, CAP - CHUNK_ROWS))
    chunks = len(bounds)

    def expert_slice(rows, gate_w, up_w, down_w):
        flat = rows.reshape(-1, model_width)
        gate = jnp.dot(flat, gate_w, preferred_element_type=jnp.float32)
        up_val = jnp.dot(flat, up_w, preferred_element_type=jnp.float32)
        hidden = ((up_val + 1.0) * gate * jax.nn.sigmoid(1.702 * gate)).astype(jnp.bfloat16)
        return jnp.dot(hidden, down_w, preferred_element_type=jnp.float32).astype(jnp.bfloat16)

    combines, received = [], []
    for first, size in bounds:
        pos = (flat_routes[:, None] * halves + jnp.arange(halves, dtype=jnp.int32)[None, :]) * size
        pos = (pos + (slot_rank - first)[:, None]).reshape(tok_rows, TOPK, halves)
        inside = ((slot_rank >= first) & (slot_rank < first + size)).reshape(tok_rows, TOPK)
        row_ids = jnp.arange(EXPERTS * halves * size, dtype=jnp.int32)
        match = (pos[:, :, :, None] == row_ids[None, None, None, :]) & inside[:, :, None, None]
        dispatch_table = jnp.any(match, axis=(1, 2)).T.astype(jnp.bfloat16)
        send_rows = jnp.dot(dispatch_table, normed2, preferred_element_type=jnp.float32).astype(
            jnp.bfloat16
        )
        if size % 8 == 0:
            send_rows = with_layout_constraint(send_rows, Layout(major_to_minor=(0, 1))).reshape(
                EXPERTS * halves, size, model_width
            )
        else:
            send_rows = send_rows.reshape(EXPERTS * halves, size * model_width)
        combines.append(jnp.sum(jnp.where(match, weights[:, :, None, None], 0.0), axis=(1, 2)))
        received.append(
            lax.all_to_all(send_rows, ("req", "y"), split_axis=0, concat_axis=0, tiled=True)
        )
    chip_sums, returned = [], []
    for part in range(chunks):
        rows = received[part]
        if part > 0:
            rows, chip_sums[-1] = lax.optimization_barrier((rows, chip_sums[-1]))
            returned.append(
                lax.all_to_all(chip_sums[-1], ("req", "y"), split_axis=0, concat_axis=0, tiled=True)
            )
        own_out = expert_slice(rows, expert_gate[0], expert_up[0], expert_down[0])
        sibling_out = expert_slice(rows, *sibling_weights)
        chip_sum = (own_out.astype(jnp.float32) + sibling_out.astype(jnp.float32)).astype(
            jnp.bfloat16
        )
        chip_sum = with_layout_constraint(chip_sum, Layout(major_to_minor=(0, 1)))
        chip_sums.append(chip_sum.reshape(rows.shape))
        if part > 0:
            returned[-1], chip_sums[-1] = lax.optimization_barrier((returned[-1], chip_sums[-1]))
    returned.append(
        lax.all_to_all(chip_sums[-1], ("req", "y"), split_axis=0, concat_axis=0, tiled=True)
    )
    moe_sum = jnp.zeros((tok_rows, model_width), jnp.float32)
    for combine, back in zip(combines, returned):
        back = back.reshape(-1, model_width)
        combine_hi = combine.astype(jnp.bfloat16)
        combine_lo = (combine - combine_hi.astype(jnp.float32)).astype(jnp.bfloat16)
        moe_sum = moe_sum + jnp.dot(combine_hi, back, preferred_element_type=jnp.float32)
        moe_sum = moe_sum + jnp.dot(combine_lo, back, preferred_element_type=jnp.float32)
    return (residual.astype(jnp.float32) + moe_sum).astype(jnp.bfloat16)


def solution(mesh):
    n_req, n_exp = mesh.devices.shape
    fine = jax.sharding.Mesh(mesh.devices.reshape(n_req, n_exp // 2, 2), ("req", "y", "c"))
    tok = ("req", "y", "c")
    return jax.shard_map(
        per_device,
        mesh=fine,
        in_specs=(
            P(tok, None),
            P(),
            P(None, ("y", "c")),
            P(None, ("y", "c")),
            P(None, ("y", "c")),
            P(("y", "c")),
            P(("y", "c"), None),
            P(),
            P(),
            P(tok, None),
            P("req", None),
            P(tok, None, None),
            P(tok, None, None),
            P(tok, None, None),
        ),
        out_specs=P(tok, None),
        check_vma=False,
    )
```

```python
import jax
import jax.numpy as jnp
from jax import lax
from jax.experimental.layout import Layout, with_layout_constraint
from jax.sharding import PartitionSpec as P

QUERY_HEADS = 64
KEY_VALUE_HEADS = 8
HEAD_DIM = 64
EXPERTS = 32
TOPK = 4
CAP = 14
ROWS = 16
CHUNK_ROWS = 8
LONGEST = 384
QUERY_BLOCKS = 4


def rms_norm(value_rows, gain):
    mean_sq = jnp.mean(value_rows * value_rows, axis=-1, keepdims=True)
    return value_rows * lax.rsqrt(mean_sq + 1e-05) * gain


def rotate(value_rows, offset):
    half = value_rows.shape[-1] // 2
    freqs = jnp.exp(
        -(2.0 * jnp.arange(half, dtype=jnp.float32) / value_rows.shape[-1])
        * jnp.log(jnp.float32(150000.0))
    )
    angle = offset.astype(jnp.float32)[:, None] * freqs[None, :]
    cosine = jnp.cos(angle)[:, None, :]
    sine = jnp.sin(angle)[:, None, :]
    first = value_rows[..., :half]
    second = value_rows[..., half:]
    return jnp.concatenate(
        [first * cosine - second * sine, second * cosine + first * sine], axis=-1
    )


def per_device(
    tokens,
    attn_gain,
    w_query,
    key_weight,
    value_weight,
    sinks,
    w_out,
    ffn_gain,
    router,
    routes,
    lengths,
    expert_gate,
    expert_up,
    expert_down,
):
    tok_rows = tokens.shape[0]
    model_width = tokens.shape[1]
    local_heads = w_query.shape[1] // HEAD_DIM
    local_kv = key_weight.shape[1] // HEAD_DIM
    head_group = QUERY_HEADS // KEY_VALUE_HEADS
    normed_input = rms_norm(tokens.astype(jnp.float32), attn_gain).astype(jnp.bfloat16)
    piece = lax.all_gather(normed_input, ("y", "c"), axis=0, tiled=True)
    projected = jnp.concatenate(
        [
            jnp.dot(piece, w_query, preferred_element_type=jnp.float32),
            jnp.dot(piece, key_weight, preferred_element_type=jnp.float32),
            jnp.dot(piece, value_weight, preferred_element_type=jnp.float32),
        ],
        axis=1,
    )
    item_count = projected.shape[0]
    lens = lengths[0]
    ends = jnp.cumsum(lens)
    starts = ends - lens
    position = jnp.arange(item_count, dtype=jnp.int32)
    member = ((position[:, None] >= starts[None, :]) & (position[:, None] < ends[None, :])).astype(
        jnp.int32
    )
    segment = jnp.sum(member * jnp.arange(lens.shape[0], dtype=jnp.int32)[None, :], axis=1)
    offset = position - jnp.sum(member * starts[None, :], axis=1)
    q_width = local_heads * HEAD_DIM
    kv_width = local_kv * HEAD_DIM
    query_rows = rotate(
        projected[:, :q_width].reshape(item_count, local_heads, HEAD_DIM), offset
    ).astype(jnp.bfloat16)
    key_rows = rotate(
        projected[:, q_width : q_width + kv_width].reshape(item_count, local_kv, HEAD_DIM), offset
    ).astype(jnp.bfloat16)
    value_rows = (
        projected[:, q_width + kv_width :]
        .reshape(item_count, local_kv, HEAD_DIM)
        .astype(jnp.bfloat16)
    )
    grouped_heads = query_rows.reshape(item_count, local_kv, head_group, HEAD_DIM)
    sink_score_logit = sinks.reshape(local_kv, head_group, 1, 1)
    block = item_count // QUERY_BLOCKS
    pieces = []
    for b in range(QUERY_BLOCKS):
        q0, q1 = b * block, (b + 1) * block
        k0 = max(0, (q0 - LONGEST + 1) // block * block)
        scores = jnp.einsum(
            "qcgd,kcd->cgqk", grouped_heads[q0:q1], key_rows[k0:q1], preferred_element_type=jnp.float32
        ) * HEAD_DIM ** (-0.5)
        allowed = (segment[q0:q1, None] == segment[None, k0:q1]) & (
            position[None, k0:q1] <= position[q0:q1, None]
        )
        masked = jnp.where(allowed[None, None], scores, -jnp.inf)
        top = jnp.maximum(jnp.max(masked, axis=-1, keepdims=True), sink_score_logit)
        expo = jnp.where(allowed[None, None], jnp.exp(scores - top), 0.0)
        denom = jnp.sum(expo, axis=-1, keepdims=True) + jnp.exp(sink_score_logit - top)
        probs = (expo / denom).astype(jnp.bfloat16)
        pieces.append(
            jnp.einsum("cgqk,kcd->qcgd", probs, value_rows[k0:q1], preferred_element_type=jnp.float32)
        )
    attended = jnp.concatenate(pieces, axis=0)
    attended = attended.reshape(item_count, q_width).astype(jnp.bfloat16)
    swap = [(0, 1), (1, 0)]
    sibling_weights = [lax.ppermute(w[0], "c", perm=swap) for w in (expert_gate, expert_up, expert_down)]
    attended, *sibling_weights = lax.optimization_barrier((attended, *sibling_weights))
    pair_gate = jnp.concatenate([expert_gate[0], sibling_weights[0]], axis=1)
    pair_up = jnp.concatenate([expert_up[0], sibling_weights[1]], axis=1)
    pair_down = jnp.concatenate([expert_down[0], sibling_weights[2]], axis=0)
    attn_sum = lax.psum_scatter(
        jnp.dot(attended, w_out, preferred_element_type=jnp.float32).astype(jnp.bfloat16),
        ("y", "c"),
        scatter_dimension=0,
        tiled=True,
    ).astype(jnp.float32)
    residual = (tokens.astype(jnp.float32) + attn_sum).astype(jnp.bfloat16)
    normed2 = rms_norm(residual.astype(jnp.float32), ffn_gain).astype(jnp.bfloat16)
    logits = jnp.dot(normed2, router, preferred_element_type=jnp.float32)
    picked = jnp.take_along_axis(logits, routes, axis=1)
    weights = jax.nn.softmax(picked, axis=-1)
    flat_routes = routes.reshape(-1)
    expert_ids = jnp.arange(EXPERTS, dtype=jnp.int32)
    onehot_route = (flat_routes[:, None] == expert_ids[None, :]).astype(jnp.int32)
    rank = jnp.cumsum(onehot_route, axis=0) - 1
    slot_rank = jnp.sum(onehot_route * rank, axis=1)
    n_y = lax.axis_size("y")
    halves = n_y // (EXPERTS // lax.axis_size("req"))
    chunks = ROWS // CHUNK_ROWS
    pos = (flat_routes[:, None] * halves + jnp.arange(halves, dtype=jnp.int32)[None, :]) * CHUNK_ROWS
    pos = (pos + (slot_rank % CHUNK_ROWS)[:, None]).reshape(tok_rows, TOPK, halves)
    part_of = (slot_rank // CHUNK_ROWS).reshape(tok_rows, TOPK)
    row_ids = jnp.arange(EXPERTS * halves * CHUNK_ROWS, dtype=jnp.int32)
    placed = pos[:, :, :, None] == row_ids[None, None, None, :]

    def expert_slice(rows, gate_w, up_w, down_w):
        flat = rows.reshape(-1, model_width)
        gate = jnp.dot(flat, gate_w, preferred_element_type=jnp.float32)
        up_val = jnp.dot(flat, up_w, preferred_element_type=jnp.float32)
        hidden = ((up_val + 1.0) * gate * jax.nn.sigmoid(1.702 * gate)).astype(jnp.bfloat16)
        return jnp.dot(hidden, down_w, preferred_element_type=jnp.float32).astype(jnp.bfloat16)

    tables, combines, received = [], [], []
    for part in range(chunks):
        match = placed & (part_of == part)[:, :, None, None]
        dispatch_table = jnp.any(match, axis=(1, 2)).T.astype(jnp.bfloat16)
        send_rows = jnp.dot(dispatch_table, normed2, preferred_element_type=jnp.float32).astype(
            jnp.bfloat16
        )
        send_rows = with_layout_constraint(send_rows, Layout(major_to_minor=(0, 1))).reshape(
            EXPERTS * halves, CHUNK_ROWS, model_width
        )
        combines.append(jnp.sum(jnp.where(match, weights[:, :, None, None], 0.0), axis=(1, 2)))
        received.append(
            lax.all_to_all(send_rows, ("req", "y"), split_axis=0, concat_axis=0, tiled=True)
        )
    chip_sums, returned = [], []
    for part in range(chunks):
        rows = received[part]
        if part > 0:
            rows, chip_sums[-1] = lax.optimization_barrier((rows, chip_sums[-1]))
            returned.append(
                lax.all_to_all(chip_sums[-1], ("req", "y"), split_axis=0, concat_axis=0, tiled=True)
            )
        chip_sum = expert_slice(rows, pair_gate, pair_up, pair_down)
        chip_sum = with_layout_constraint(chip_sum, Layout(major_to_minor=(0, 1)))
        chip_sums.append(chip_sum.reshape(rows.shape))
        if part > 0:
            returned[-1], chip_sums[-1] = lax.optimization_barrier((returned[-1], chip_sums[-1]))
    returned.append(
        lax.all_to_all(chip_sums[-1], ("req", "y"), split_axis=0, concat_axis=0, tiled=True)
    )
    moe_sum = jnp.zeros((tok_rows, model_width), jnp.float32)
    for combine, back in zip(combines, returned):
        back = back.reshape(-1, model_width)
        combine_hi = combine.astype(jnp.bfloat16)
        combine_lo = (combine - combine_hi.astype(jnp.float32)).astype(jnp.bfloat16)
        moe_sum = moe_sum + jnp.dot(combine_hi, back, preferred_element_type=jnp.float32)
        moe_sum = moe_sum + jnp.dot(combine_lo, back, preferred_element_type=jnp.float32)
    return (residual.astype(jnp.float32) + moe_sum).astype(jnp.bfloat16)


def solution(mesh):
    n_req, n_exp = mesh.devices.shape
    fine = jax.sharding.Mesh(mesh.devices.reshape(n_req, n_exp // 2, 2), ("req", "y", "c"))
    tok = ("req", "y", "c")
    return jax.shard_map(
        per_device,
        mesh=fine,
        in_specs=(
            P(tok, None),
            P(),
            P(None, ("y", "c")),
            P(None, ("y", "c")),
            P(None, ("y", "c")),
            P(("y", "c")),
            P(("y", "c"), None),
            P(),
            P(),
            P(tok, None),
            P("req", None),
            P(tok, None, None),
            P(tok, None, None),
            P(tok, None, None),
        ),
        out_specs=P(tok, None),
        check_vma=False,
    )
```

```python
import jax
import jax.numpy as jnp
from jax import lax
from jax.experimental.layout import Layout, with_layout_constraint
from jax.sharding import PartitionSpec as P

QUERY_HEADS = 64
KEY_VALUE_HEADS = 8
HEAD_DIM = 64
EXPERTS = 32
TOPK = 4
CAP = 14
ROWS = 16
CHUNK_ROWS = 8
LONGEST = 384
QUERY_BLOCKS = 4


def rms_norm(value_rows, gain):
    mean_sq = jnp.mean(value_rows * value_rows, axis=-1, keepdims=True)
    return value_rows * lax.rsqrt(mean_sq + 1e-05) * gain


def rotate(value_rows, offset):
    half = value_rows.shape[-1] // 2
    freqs = jnp.exp(
        -(2.0 * jnp.arange(half, dtype=jnp.float32) / value_rows.shape[-1])
        * jnp.log(jnp.float32(150000.0))
    )
    angle = offset.astype(jnp.float32)[:, None] * freqs[None, :]
    cosine = jnp.cos(angle)[:, None, :]
    sine = jnp.sin(angle)[:, None, :]
    first = value_rows[..., :half]
    second = value_rows[..., half:]
    return jnp.concatenate(
        [first * cosine - second * sine, second * cosine + first * sine], axis=-1
    )


def per_device(
    tokens,
    attn_gain,
    w_query,
    key_weight,
    value_weight,
    sinks,
    w_out,
    ffn_gain,
    router,
    routes,
    lengths,
    expert_gate,
    expert_up,
    expert_down,
):
    tok_rows = tokens.shape[0]
    model_width = tokens.shape[1]
    local_heads = w_query.shape[1] // HEAD_DIM
    local_kv = key_weight.shape[1] // HEAD_DIM
    head_group = QUERY_HEADS // KEY_VALUE_HEADS
    normed_input = rms_norm(tokens.astype(jnp.float32), attn_gain).astype(jnp.bfloat16)
    piece = lax.all_gather(normed_input, ("y", "c"), axis=0, tiled=True)
    projected = jnp.concatenate(
        [
            jnp.dot(piece, w_query, preferred_element_type=jnp.float32),
            jnp.dot(piece, key_weight, preferred_element_type=jnp.float32),
            jnp.dot(piece, value_weight, preferred_element_type=jnp.float32),
        ],
        axis=1,
    )
    item_count = projected.shape[0]
    lens = lengths[0]
    ends = jnp.cumsum(lens)
    starts = ends - lens
    position = jnp.arange(item_count, dtype=jnp.int32)
    member = ((position[:, None] >= starts[None, :]) & (position[:, None] < ends[None, :])).astype(
        jnp.int32
    )
    segment = jnp.sum(member * jnp.arange(lens.shape[0], dtype=jnp.int32)[None, :], axis=1)
    offset = position - jnp.sum(member * starts[None, :], axis=1)
    q_width = local_heads * HEAD_DIM
    kv_width = local_kv * HEAD_DIM
    query_rows = rotate(
        projected[:, :q_width].reshape(item_count, local_heads, HEAD_DIM), offset
    ).astype(jnp.bfloat16)
    key_rows = rotate(
        projected[:, q_width : q_width + kv_width].reshape(item_count, local_kv, HEAD_DIM), offset
    ).astype(jnp.bfloat16)
    value_rows = (
        projected[:, q_width + kv_width :]
        .reshape(item_count, local_kv, HEAD_DIM)
        .astype(jnp.bfloat16)
    )
    grouped_heads = query_rows.reshape(item_count, local_kv, head_group, HEAD_DIM)
    sink_score_logit = sinks.reshape(local_kv, head_group, 1, 1)
    block = item_count // QUERY_BLOCKS
    pieces = []
    for b in range(QUERY_BLOCKS):
        q0, q1 = b * block, (b + 1) * block
        k0 = max(0, (q0 - LONGEST + 1) // block * block)
        scores = jnp.einsum(
            "qcgd,kcd->cgqk", grouped_heads[q0:q1], key_rows[k0:q1], preferred_element_type=jnp.float32
        ) * HEAD_DIM ** (-0.5)
        allowed = (segment[q0:q1, None] == segment[None, k0:q1]) & (
            position[None, k0:q1] <= position[q0:q1, None]
        )
        masked = jnp.where(allowed[None, None], scores, -jnp.inf)
        top = jnp.maximum(jnp.max(masked, axis=-1, keepdims=True), sink_score_logit)
        expo = jnp.where(allowed[None, None], jnp.exp(scores - top), 0.0)
        denom = jnp.sum(expo, axis=-1, keepdims=True) + jnp.exp(sink_score_logit - top)
        probs = (expo / denom).astype(jnp.bfloat16)
        pieces.append(
            jnp.einsum("cgqk,kcd->qcgd", probs, value_rows[k0:q1], preferred_element_type=jnp.float32)
        )
    attended = jnp.concatenate(pieces, axis=0)
    attended = attended.reshape(item_count, q_width).astype(jnp.bfloat16)
    swap = [(0, 1), (1, 0)]
    sibling_weights = [lax.ppermute(w[0], "c", perm=swap) for w in (expert_gate, expert_up, expert_down)]
    attended, *sibling_weights = lax.optimization_barrier((attended, *sibling_weights))
    pair_gate = jnp.concatenate([expert_gate[0], sibling_weights[0]], axis=1)
    pair_up = jnp.concatenate([expert_up[0], sibling_weights[1]], axis=1)
    pair_down = jnp.concatenate([expert_down[0], sibling_weights[2]], axis=0)
    attn_sum = lax.psum_scatter(
        jnp.dot(attended, w_out, preferred_element_type=jnp.float32).astype(jnp.bfloat16),
        ("y", "c"),
        scatter_dimension=0,
        tiled=True,
    ).astype(jnp.float32)
    residual = (tokens.astype(jnp.float32) + attn_sum).astype(jnp.bfloat16)
    normed2 = rms_norm(residual.astype(jnp.float32), ffn_gain).astype(jnp.bfloat16)
    logits = jnp.dot(normed2, router, preferred_element_type=jnp.float32)
    picked = jnp.take_along_axis(logits, routes, axis=1)
    weights = jax.nn.softmax(picked, axis=-1)
    flat_routes = routes.reshape(-1)
    expert_ids = jnp.arange(EXPERTS, dtype=jnp.int32)
    onehot_route = (flat_routes[:, None] == expert_ids[None, :]).astype(jnp.int32)
    rank = jnp.cumsum(onehot_route, axis=0) - 1
    slot_rank = jnp.sum(onehot_route * rank, axis=1)
    n_y = lax.axis_size("y")
    halves = n_y // (EXPERTS // lax.axis_size("req"))
    chunks = ROWS // CHUNK_ROWS
    pos = (flat_routes[:, None] * halves + jnp.arange(halves, dtype=jnp.int32)[None, :]) * CHUNK_ROWS
    pos = (pos + (slot_rank % CHUNK_ROWS)[:, None]).reshape(tok_rows, TOPK, halves)
    part_of = (slot_rank // CHUNK_ROWS).reshape(tok_rows, TOPK)
    row_ids = jnp.arange(EXPERTS * halves * CHUNK_ROWS, dtype=jnp.int32)
    placed = pos[:, :, :, None] == row_ids[None, None, None, :]

    def expert_slice(rows, gate_w, up_w, down_w):
        flat = rows.reshape(-1, model_width)
        gate = jnp.dot(flat, gate_w, preferred_element_type=jnp.float32)
        up_val = jnp.dot(flat, up_w, preferred_element_type=jnp.float32)
        hidden = ((up_val + 1.0) * gate * jax.nn.sigmoid(1.702 * gate)).astype(jnp.bfloat16)
        return jnp.dot(hidden, down_w, preferred_element_type=jnp.float32).astype(jnp.bfloat16)

    tables, combines, received = [], [], []
    for part in range(chunks):
        match = placed & (part_of == part)[:, :, None, None]
        dispatch_table = jnp.any(match, axis=(1, 2)).T.astype(jnp.bfloat16)
        send_rows = jnp.dot(dispatch_table, normed2, preferred_element_type=jnp.float32).astype(
            jnp.bfloat16
        )
        send_rows = with_layout_constraint(send_rows, Layout(major_to_minor=(0, 1))).reshape(
            EXPERTS * halves, CHUNK_ROWS, model_width
        )
        combines.append(jnp.sum(jnp.where(match, weights[:, :, None, None], 0.0), axis=(1, 2)))
        received.append(
            lax.all_to_all(send_rows, ("req", "y"), split_axis=0, concat_axis=0, tiled=True)
        )
    chip_sums, returned = [], []
    for part in range(chunks):
        rows = received[part]
        if part > 0:
            rows, chip_sums[-1] = lax.optimization_barrier((rows, chip_sums[-1]))
            returned.append(
                lax.all_to_all(chip_sums[-1], ("req", "y"), split_axis=0, concat_axis=0, tiled=True)
            )
        chip_sum = expert_slice(rows, pair_gate, pair_up, pair_down)
        chip_sum = with_layout_constraint(chip_sum, Layout(major_to_minor=(0, 1)))
        chip_sums.append(chip_sum.reshape(rows.shape))
        if part > 0:
            returned[-1], chip_sums[-1] = lax.optimization_barrier((returned[-1], chip_sums[-1]))
    returned.append(
        lax.all_to_all(chip_sums[-1], ("req", "y"), split_axis=0, concat_axis=0, tiled=True)
    )
    moe_sum = residual.astype(jnp.float32)
    for combine, back in zip(combines, returned):
        back = back.reshape(-1, model_width)
        combine_hi = combine.astype(jnp.bfloat16)
        combine_lo = (combine - combine_hi.astype(jnp.float32)).astype(jnp.bfloat16)
        both = jnp.dot(
            jnp.concatenate([combine_hi, combine_lo], axis=0), back, preferred_element_type=jnp.float32
        )
        moe_sum = moe_sum + (both[:tok_rows] + both[tok_rows:])
    return moe_sum.astype(jnp.bfloat16)


def solution(mesh):
    n_req, n_exp = mesh.devices.shape
    fine = jax.sharding.Mesh(mesh.devices.reshape(n_req, n_exp // 2, 2), ("req", "y", "c"))
    tok = ("req", "y", "c")
    return jax.shard_map(
        per_device,
        mesh=fine,
        in_specs=(
            P(tok, None),
            P(),
            P(None, ("y", "c")),
            P(None, ("y", "c")),
            P(None, ("y", "c")),
            P(("y", "c")),
            P(("y", "c"), None),
            P(),
            P(),
            P(tok, None),
            P("req", None),
            P(tok, None, None),
            P(tok, None, None),
            P(tok, None, None),
        ),
        out_specs=P(tok, None),
        check_vma=False,
    )
```

```python
import jax
import jax.numpy as jnp
from jax import lax
from jax.experimental.layout import Layout, with_layout_constraint
from jax.sharding import PartitionSpec as P

QUERY_HEADS = 64
KEY_VALUE_HEADS = 8
HEAD_DIM = 64
EXPERTS = 32
TOPK = 4
CAP = 14
ROWS = 16
CHUNK_ROWS = 8
LONGEST = 384
QUERY_BLOCKS = 4


def rms_norm(value_rows, gain):
    mean_sq = jnp.mean(value_rows * value_rows, axis=-1, keepdims=True)
    return value_rows * lax.rsqrt(mean_sq + 1e-05) * gain


def rotate(value_rows, offset):
    half = value_rows.shape[-1] // 2
    freqs = jnp.exp(
        -(2.0 * jnp.arange(half, dtype=jnp.float32) / value_rows.shape[-1])
        * jnp.log(jnp.float32(150000.0))
    )
    angle = offset.astype(jnp.float32)[:, None] * freqs[None, :]
    cosine = jnp.cos(angle)[:, None, :]
    sine = jnp.sin(angle)[:, None, :]
    first = value_rows[..., :half]
    second = value_rows[..., half:]
    return jnp.concatenate(
        [first * cosine - second * sine, second * cosine + first * sine], axis=-1
    )


def per_device(
    tokens,
    attn_gain,
    w_query,
    key_weight,
    value_weight,
    sinks,
    w_out,
    ffn_gain,
    router,
    routes,
    lengths,
    expert_gate,
    expert_up,
    expert_down,
):
    tok_rows = tokens.shape[0]
    model_width = tokens.shape[1]
    local_heads = w_query.shape[1] // HEAD_DIM
    local_kv = key_weight.shape[1] // HEAD_DIM
    head_group = QUERY_HEADS // KEY_VALUE_HEADS
    normed_input = rms_norm(tokens.astype(jnp.float32), attn_gain).astype(jnp.bfloat16)
    piece = lax.all_gather(normed_input, ("y", "c"), axis=0, tiled=True)
    qkv_weight = jnp.concatenate([w_query, key_weight, value_weight], axis=1)
    projected = jnp.dot(piece, qkv_weight, preferred_element_type=jnp.float32)
    item_count = projected.shape[0]
    lens = lengths[0]
    ends = jnp.cumsum(lens)
    starts = ends - lens
    position = jnp.arange(item_count, dtype=jnp.int32)
    member = ((position[:, None] >= starts[None, :]) & (position[:, None] < ends[None, :])).astype(
        jnp.int32
    )
    segment = jnp.sum(member * jnp.arange(lens.shape[0], dtype=jnp.int32)[None, :], axis=1)
    offset = position - jnp.sum(member * starts[None, :], axis=1)
    q_width = local_heads * HEAD_DIM
    kv_width = local_kv * HEAD_DIM
    query_rows = rotate(
        projected[:, :q_width].reshape(item_count, local_heads, HEAD_DIM), offset
    ).astype(jnp.bfloat16)
    key_rows = rotate(
        projected[:, q_width : q_width + kv_width].reshape(item_count, local_kv, HEAD_DIM), offset
    ).astype(jnp.bfloat16)
    value_rows = (
        projected[:, q_width + kv_width :]
        .reshape(item_count, local_kv, HEAD_DIM)
        .astype(jnp.bfloat16)
    )
    grouped_heads = query_rows.reshape(item_count, local_kv, head_group, HEAD_DIM)
    sink_score_logit = sinks.reshape(local_kv, head_group, 1, 1)
    block = item_count // QUERY_BLOCKS
    pieces = []
    for b in range(QUERY_BLOCKS):
        q0, q1 = b * block, (b + 1) * block
        k0 = max(0, (q0 - LONGEST + 1) // block * block)
        scores = jnp.einsum(
            "qcgd,kcd->cgqk", grouped_heads[q0:q1], key_rows[k0:q1], preferred_element_type=jnp.float32
        ) * HEAD_DIM ** (-0.5)
        allowed = (segment[q0:q1, None] == segment[None, k0:q1]) & (
            position[None, k0:q1] <= position[q0:q1, None]
        )
        masked = jnp.where(allowed[None, None], scores, -jnp.inf)
        top = jnp.maximum(jnp.max(masked, axis=-1, keepdims=True), sink_score_logit)
        expo = jnp.where(allowed[None, None], jnp.exp(scores - top), 0.0)
        denom = jnp.sum(expo, axis=-1, keepdims=True) + jnp.exp(sink_score_logit - top)
        probs = (expo / denom).astype(jnp.bfloat16)
        pieces.append(
            jnp.einsum("cgqk,kcd->qcgd", probs, value_rows[k0:q1], preferred_element_type=jnp.float32)
        )
    attended = jnp.concatenate(pieces, axis=0)
    attended = attended.reshape(item_count, q_width).astype(jnp.bfloat16)
    swap = [(0, 1), (1, 0)]
    sibling_weights = [lax.ppermute(w[0], "c", perm=swap) for w in (expert_gate, expert_up, expert_down)]
    attended, *sibling_weights = lax.optimization_barrier((attended, *sibling_weights))
    pair_gate = jnp.concatenate([expert_gate[0], sibling_weights[0]], axis=1)
    pair_up = jnp.concatenate([expert_up[0], sibling_weights[1]], axis=1)
    pair_down = jnp.concatenate([expert_down[0], sibling_weights[2]], axis=0)
    attn_sum = lax.psum_scatter(
        jnp.dot(attended, w_out, preferred_element_type=jnp.float32).astype(jnp.bfloat16),
        ("y", "c"),
        scatter_dimension=0,
        tiled=True,
    ).astype(jnp.float32)
    residual = (tokens.astype(jnp.float32) + attn_sum).astype(jnp.bfloat16)
    normed2 = rms_norm(residual.astype(jnp.float32), ffn_gain).astype(jnp.bfloat16)
    logits = jnp.dot(normed2, router, preferred_element_type=jnp.float32)
    picked = jnp.take_along_axis(logits, routes, axis=1)
    weights = jax.nn.softmax(picked, axis=-1)
    flat_routes = routes.reshape(-1)
    expert_ids = jnp.arange(EXPERTS, dtype=jnp.int32)
    onehot_route = (flat_routes[:, None] == expert_ids[None, :]).astype(jnp.int32)
    rank = jnp.cumsum(onehot_route, axis=0) - 1
    slot_rank = jnp.sum(onehot_route * rank, axis=1)
    n_y = lax.axis_size("y")
    halves = n_y // (EXPERTS // lax.axis_size("req"))
    chunks = ROWS // CHUNK_ROWS
    pos = (flat_routes[:, None] * halves + jnp.arange(halves, dtype=jnp.int32)[None, :]) * CHUNK_ROWS
    pos = (pos + (slot_rank % CHUNK_ROWS)[:, None]).reshape(tok_rows, TOPK, halves)
    part_of = (slot_rank // CHUNK_ROWS).reshape(tok_rows, TOPK)
    row_ids = jnp.arange(EXPERTS * halves * CHUNK_ROWS, dtype=jnp.int32)
    placed = pos[:, :, :, None] == row_ids[None, None, None, :]

    def expert_slice(rows, gate_w, up_w, down_w):
        flat = rows.reshape(-1, model_width)
        gate = jnp.dot(flat, gate_w, preferred_element_type=jnp.float32)
        up_val = jnp.dot(flat, up_w, preferred_element_type=jnp.float32)
        hidden = ((up_val + 1.0) * gate * jax.nn.sigmoid(1.702 * gate)).astype(jnp.bfloat16)
        return jnp.dot(hidden, down_w, preferred_element_type=jnp.float32).astype(jnp.bfloat16)

    tables, combines, received = [], [], []
    for part in range(chunks):
        match = placed & (part_of == part)[:, :, None, None]
        dispatch_table = jnp.any(match, axis=(1, 2)).T.astype(jnp.bfloat16)
        send_rows = jnp.dot(dispatch_table, normed2, preferred_element_type=jnp.float32).astype(
            jnp.bfloat16
        )
        send_rows = with_layout_constraint(send_rows, Layout(major_to_minor=(0, 1))).reshape(
            EXPERTS * halves, CHUNK_ROWS, model_width
        )
        combines.append(jnp.sum(jnp.where(match, weights[:, :, None, None], 0.0), axis=(1, 2)))
        received.append(
            lax.all_to_all(send_rows, ("req", "y"), split_axis=0, concat_axis=0, tiled=True)
        )
    chip_sums, returned = [], []
    for part in range(chunks):
        rows = received[part]
        if part > 0:
            rows, chip_sums[-1] = lax.optimization_barrier((rows, chip_sums[-1]))
            returned.append(
                lax.all_to_all(chip_sums[-1], ("req", "y"), split_axis=0, concat_axis=0, tiled=True)
            )
        chip_sum = expert_slice(rows, pair_gate, pair_up, pair_down)
        chip_sum = with_layout_constraint(chip_sum, Layout(major_to_minor=(0, 1)))
        chip_sums.append(chip_sum.reshape(rows.shape))
        if part > 0:
            returned[-1], chip_sums[-1] = lax.optimization_barrier((returned[-1], chip_sums[-1]))
    returned.append(
        lax.all_to_all(chip_sums[-1], ("req", "y"), split_axis=0, concat_axis=0, tiled=True)
    )
    moe_sum = residual.astype(jnp.float32)
    for combine, back in zip(combines, returned):
        back = back.reshape(-1, model_width)
        combine_hi = combine.astype(jnp.bfloat16)
        combine_lo = (combine - combine_hi.astype(jnp.float32)).astype(jnp.bfloat16)
        both = jnp.dot(
            jnp.concatenate([combine_hi, combine_lo], axis=0), back, preferred_element_type=jnp.float32
        )
        moe_sum = moe_sum + (both[:tok_rows] + both[tok_rows:])
    return moe_sum.astype(jnp.bfloat16)


def solution(mesh):
    n_req, n_exp = mesh.devices.shape
    fine = jax.sharding.Mesh(mesh.devices.reshape(n_req, n_exp // 2, 2), ("req", "y", "c"))
    tok = ("req", "y", "c")
    return jax.shard_map(
        per_device,
        mesh=fine,
        in_specs=(
            P(tok, None),
            P(),
            P(None, ("y", "c")),
            P(None, ("y", "c")),
            P(None, ("y", "c")),
            P(("y", "c")),
            P(("y", "c"), None),
            P(),
            P(),
            P(tok, None),
            P("req", None),
            P(tok, None, None),
            P(tok, None, None),
            P(tok, None, None),
        ),
        out_specs=P(tok, None),
        check_vma=False,
    )
```

```python
import jax
import jax.numpy as jnp
from jax import lax
from jax.experimental.layout import Layout, with_layout_constraint
from jax.sharding import PartitionSpec as P

QUERY_HEADS = 64
KEY_VALUE_HEADS = 8
HEAD_DIM = 64
EXPERTS = 32
TOPK = 4
CAP = 14
ROWS = 16
CHUNK_ROWS = 8
LONGEST = 384
QUERY_BLOCKS = 4


def rms_norm(value_rows, gain):
    mean_sq = jnp.mean(value_rows * value_rows, axis=-1, keepdims=True)
    return value_rows * lax.rsqrt(mean_sq + 1e-05) * gain


def rotate(value_rows, offset):
    half = value_rows.shape[-1] // 2
    freqs = jnp.exp(
        -(2.0 * jnp.arange(half, dtype=jnp.float32) / value_rows.shape[-1])
        * jnp.log(jnp.float32(150000.0))
    )
    angle = offset.astype(jnp.float32)[:, None] * freqs[None, :]
    cosine = jnp.cos(angle)[:, None, :]
    sine = jnp.sin(angle)[:, None, :]
    first = value_rows[..., :half]
    second = value_rows[..., half:]
    return jnp.concatenate(
        [first * cosine - second * sine, second * cosine + first * sine], axis=-1
    )


def per_device(
    tokens,
    attn_gain,
    w_query,
    key_weight,
    value_weight,
    sinks,
    w_out,
    ffn_gain,
    router,
    routes,
    lengths,
    expert_gate,
    expert_up,
    expert_down,
):
    tok_rows = tokens.shape[0]
    model_width = tokens.shape[1]
    local_heads = w_query.shape[1] // HEAD_DIM
    local_kv = key_weight.shape[1] // HEAD_DIM
    head_group = QUERY_HEADS // KEY_VALUE_HEADS
    gathered = lax.all_gather(tokens, ("y", "c"), axis=0, tiled=True)
    piece = rms_norm(gathered.astype(jnp.float32), attn_gain).astype(jnp.bfloat16)
    qkv_weight = jnp.concatenate([w_query, key_weight, value_weight], axis=1)
    projected = jnp.dot(piece, qkv_weight, preferred_element_type=jnp.float32)
    item_count = projected.shape[0]
    lens = lengths[0]
    ends = jnp.cumsum(lens)
    starts = ends - lens
    position = jnp.arange(item_count, dtype=jnp.int32)
    member = ((position[:, None] >= starts[None, :]) & (position[:, None] < ends[None, :])).astype(
        jnp.int32
    )
    segment = jnp.sum(member * jnp.arange(lens.shape[0], dtype=jnp.int32)[None, :], axis=1)
    offset = position - jnp.sum(member * starts[None, :], axis=1)
    q_width = local_heads * HEAD_DIM
    kv_width = local_kv * HEAD_DIM
    query_rows = rotate(
        projected[:, :q_width].reshape(item_count, local_heads, HEAD_DIM), offset
    ).astype(jnp.bfloat16)
    key_rows = rotate(
        projected[:, q_width : q_width + kv_width].reshape(item_count, local_kv, HEAD_DIM), offset
    ).astype(jnp.bfloat16)
    value_rows = (
        projected[:, q_width + kv_width :]
        .reshape(item_count, local_kv, HEAD_DIM)
        .astype(jnp.bfloat16)
    )
    grouped_heads = query_rows.reshape(item_count, local_kv, head_group, HEAD_DIM)
    sink_score_logit = sinks.reshape(local_kv, head_group, 1, 1)
    block = item_count // QUERY_BLOCKS
    pieces = []
    for b in range(QUERY_BLOCKS):
        q0, q1 = b * block, (b + 1) * block
        k0 = max(0, (q0 - LONGEST + 1) // block * block)
        scores = jnp.einsum(
            "qcgd,kcd->cgqk", grouped_heads[q0:q1], key_rows[k0:q1], preferred_element_type=jnp.float32
        ) * HEAD_DIM ** (-0.5)
        allowed = (segment[q0:q1, None] == segment[None, k0:q1]) & (
            position[None, k0:q1] <= position[q0:q1, None]
        )
        masked = jnp.where(allowed[None, None], scores, -jnp.inf)
        top = jnp.maximum(jnp.max(masked, axis=-1, keepdims=True), sink_score_logit)
        expo = jnp.where(allowed[None, None], jnp.exp(scores - top), 0.0)
        denom = jnp.sum(expo, axis=-1, keepdims=True) + jnp.exp(sink_score_logit - top)
        probs = (expo / denom).astype(jnp.bfloat16)
        pieces.append(
            jnp.einsum("cgqk,kcd->qcgd", probs, value_rows[k0:q1], preferred_element_type=jnp.float32)
        )
    attended = jnp.concatenate(pieces, axis=0)
    attended = attended.reshape(item_count, q_width).astype(jnp.bfloat16)
    swap = [(0, 1), (1, 0)]
    sibling_weights = [lax.ppermute(w[0], "c", perm=swap) for w in (expert_gate, expert_up, expert_down)]
    attended, *sibling_weights = lax.optimization_barrier((attended, *sibling_weights))
    pair_gate = jnp.concatenate([expert_gate[0], sibling_weights[0]], axis=1)
    pair_up = jnp.concatenate([expert_up[0], sibling_weights[1]], axis=1)
    pair_down = jnp.concatenate([expert_down[0], sibling_weights[2]], axis=0)
    attn_sum = lax.psum_scatter(
        jnp.dot(attended, w_out, preferred_element_type=jnp.float32).astype(jnp.bfloat16),
        ("y", "c"),
        scatter_dimension=0,
        tiled=True,
    ).astype(jnp.float32)
    residual = (tokens.astype(jnp.float32) + attn_sum).astype(jnp.bfloat16)
    normed2 = rms_norm(residual.astype(jnp.float32), ffn_gain).astype(jnp.bfloat16)
    logits = jnp.dot(normed2, router, preferred_element_type=jnp.float32)
    picked = jnp.take_along_axis(logits, routes, axis=1)
    weights = jax.nn.softmax(picked, axis=-1)
    flat_routes = routes.reshape(-1)
    expert_ids = jnp.arange(EXPERTS, dtype=jnp.int32)
    onehot_route = (flat_routes[:, None] == expert_ids[None, :]).astype(jnp.int32)
    rank = jnp.cumsum(onehot_route, axis=0) - 1
    slot_rank = jnp.sum(onehot_route * rank, axis=1)
    n_y = lax.axis_size("y")
    halves = n_y // (EXPERTS // lax.axis_size("req"))
    chunks = ROWS // CHUNK_ROWS
    pos = (flat_routes[:, None] * halves + jnp.arange(halves, dtype=jnp.int32)[None, :]) * CHUNK_ROWS
    pos = (pos + (slot_rank % CHUNK_ROWS)[:, None]).reshape(tok_rows, TOPK, halves)
    part_of = (slot_rank // CHUNK_ROWS).reshape(tok_rows, TOPK)
    row_ids = jnp.arange(EXPERTS * halves * CHUNK_ROWS, dtype=jnp.int32)
    placed = pos[:, :, :, None] == row_ids[None, None, None, :]

    def expert_slice(rows, gate_w, up_w, down_w):
        flat = rows.reshape(-1, model_width)
        gate = jnp.dot(flat, gate_w, preferred_element_type=jnp.float32)
        up_val = jnp.dot(flat, up_w, preferred_element_type=jnp.float32)
        hidden = ((up_val + 1.0) * gate * jax.nn.sigmoid(1.702 * gate)).astype(jnp.bfloat16)
        return jnp.dot(hidden, down_w, preferred_element_type=jnp.float32).astype(jnp.bfloat16)

    tables, combines, received = [], [], []
    for part in range(chunks):
        match = placed & (part_of == part)[:, :, None, None]
        dispatch_table = jnp.any(match, axis=(1, 2)).T.astype(jnp.bfloat16)
        send_rows = jnp.dot(dispatch_table, normed2, preferred_element_type=jnp.float32).astype(
            jnp.bfloat16
        )
        send_rows = with_layout_constraint(send_rows, Layout(major_to_minor=(0, 1))).reshape(
            EXPERTS * halves, CHUNK_ROWS, model_width
        )
        combines.append(jnp.sum(jnp.where(match, weights[:, :, None, None], 0.0), axis=(1, 2)))
        received.append(
            lax.all_to_all(send_rows, ("req", "y"), split_axis=0, concat_axis=0, tiled=True)
        )
    chip_sums, returned = [], []
    for part in range(chunks):
        rows = received[part]
        if part > 0:
            rows, chip_sums[-1] = lax.optimization_barrier((rows, chip_sums[-1]))
            returned.append(
                lax.all_to_all(chip_sums[-1], ("req", "y"), split_axis=0, concat_axis=0, tiled=True)
            )
        chip_sum = expert_slice(rows, pair_gate, pair_up, pair_down)
        chip_sum = with_layout_constraint(chip_sum, Layout(major_to_minor=(0, 1)))
        chip_sums.append(chip_sum.reshape(rows.shape))
        if part > 0:
            returned[-1], chip_sums[-1] = lax.optimization_barrier((returned[-1], chip_sums[-1]))
    returned.append(
        lax.all_to_all(chip_sums[-1], ("req", "y"), split_axis=0, concat_axis=0, tiled=True)
    )
    moe_sum = residual.astype(jnp.float32)
    for combine, back in zip(combines, returned):
        back = back.reshape(-1, model_width)
        combine_hi = combine.astype(jnp.bfloat16)
        combine_lo = (combine - combine_hi.astype(jnp.float32)).astype(jnp.bfloat16)
        both = jnp.dot(
            jnp.concatenate([combine_hi, combine_lo], axis=0), back, preferred_element_type=jnp.float32
        )
        moe_sum = moe_sum + (both[:tok_rows] + both[tok_rows:])
    return moe_sum.astype(jnp.bfloat16)


def solution(mesh):
    n_req, n_exp = mesh.devices.shape
    fine = jax.sharding.Mesh(mesh.devices.reshape(n_req, n_exp // 2, 2), ("req", "y", "c"))
    tok = ("req", "y", "c")
    return jax.shard_map(
        per_device,
        mesh=fine,
        in_specs=(
            P(tok, None),
            P(),
            P(None, ("y", "c")),
            P(None, ("y", "c")),
            P(None, ("y", "c")),
            P(("y", "c")),
            P(("y", "c"), None),
            P(),
            P(),
            P(tok, None),
            P("req", None),
            P(tok, None, None),
            P(tok, None, None),
            P(tok, None, None),
        ),
        out_specs=P(tok, None),
        check_vma=False,
    )
```

```python
import jax
import jax.numpy as jnp
from jax import lax
from jax.experimental.layout import Layout, with_layout_constraint
from jax.sharding import PartitionSpec as P

QUERY_HEADS = 64
KEY_VALUE_HEADS = 8
HEAD_DIM = 64
EXPERTS = 32
TOPK = 4
CAP = 14
ROWS = 16
CHUNK_ROWS = 8
LONGEST = 384
QUERY_BLOCKS = 6


def rms_norm(value_rows, gain):
    mean_sq = jnp.mean(value_rows * value_rows, axis=-1, keepdims=True)
    return value_rows * lax.rsqrt(mean_sq + 1e-05) * gain


def rotate(value_rows, offset):
    half = value_rows.shape[-1] // 2
    freqs = jnp.exp(
        -(2.0 * jnp.arange(half, dtype=jnp.float32) / value_rows.shape[-1])
        * jnp.log(jnp.float32(150000.0))
    )
    angle = offset.astype(jnp.float32)[:, None] * freqs[None, :]
    cosine = jnp.cos(angle)[:, None, :]
    sine = jnp.sin(angle)[:, None, :]
    first = value_rows[..., :half]
    second = value_rows[..., half:]
    return jnp.concatenate(
        [first * cosine - second * sine, second * cosine + first * sine], axis=-1
    )


def per_device(
    tokens,
    attn_gain,
    w_query,
    key_weight,
    value_weight,
    sinks,
    w_out,
    ffn_gain,
    router,
    routes,
    lengths,
    expert_gate,
    expert_up,
    expert_down,
):
    tok_rows = tokens.shape[0]
    model_width = tokens.shape[1]
    local_heads = w_query.shape[1] // HEAD_DIM
    local_kv = key_weight.shape[1] // HEAD_DIM
    head_group = QUERY_HEADS // KEY_VALUE_HEADS
    normed_input = rms_norm(tokens.astype(jnp.float32), attn_gain).astype(jnp.bfloat16)
    piece = lax.all_gather(normed_input, ("y", "c"), axis=0, tiled=True)
    qkv_weight = jnp.concatenate([w_query, key_weight, value_weight], axis=1)
    projected = jnp.dot(piece, qkv_weight, preferred_element_type=jnp.float32)
    item_count = projected.shape[0]
    lens = lengths[0]
    ends = jnp.cumsum(lens)
    starts = ends - lens
    position = jnp.arange(item_count, dtype=jnp.int32)
    member = ((position[:, None] >= starts[None, :]) & (position[:, None] < ends[None, :])).astype(
        jnp.int32
    )
    segment = jnp.sum(member * jnp.arange(lens.shape[0], dtype=jnp.int32)[None, :], axis=1)
    offset = position - jnp.sum(member * starts[None, :], axis=1)
    q_width = local_heads * HEAD_DIM
    kv_width = local_kv * HEAD_DIM
    query_rows = rotate(
        projected[:, :q_width].reshape(item_count, local_heads, HEAD_DIM), offset
    ).astype(jnp.bfloat16)
    key_rows = rotate(
        projected[:, q_width : q_width + kv_width].reshape(item_count, local_kv, HEAD_DIM), offset
    ).astype(jnp.bfloat16)
    value_rows = (
        projected[:, q_width + kv_width :]
        .reshape(item_count, local_kv, HEAD_DIM)
        .astype(jnp.bfloat16)
    )
    grouped_heads = query_rows.reshape(item_count, local_kv, head_group, HEAD_DIM)
    sink_score_logit = sinks.reshape(local_kv, head_group, 1, 1)
    block = item_count // QUERY_BLOCKS
    pieces = []
    for b in range(QUERY_BLOCKS):
        q0, q1 = b * block, (b + 1) * block
        k0 = max(0, (q0 - LONGEST + 1) // block * block)
        scores = jnp.einsum(
            "qcgd,kcd->cgqk", grouped_heads[q0:q1], key_rows[k0:q1], preferred_element_type=jnp.float32
        ) * HEAD_DIM ** (-0.5)
        allowed = (segment[q0:q1, None] == segment[None, k0:q1]) & (
            position[None, k0:q1] <= position[q0:q1, None]
        )
        masked = jnp.where(allowed[None, None], scores, -jnp.inf)
        top = jnp.maximum(jnp.max(masked, axis=-1, keepdims=True), sink_score_logit)
        expo = jnp.where(allowed[None, None], jnp.exp(scores - top), 0.0)
        denom = jnp.sum(expo, axis=-1, keepdims=True) + jnp.exp(sink_score_logit - top)
        probs = (expo / denom).astype(jnp.bfloat16)
        pieces.append(
            jnp.einsum("cgqk,kcd->qcgd", probs, value_rows[k0:q1], preferred_element_type=jnp.float32)
        )
    attended = jnp.concatenate(pieces, axis=0)
    attended = attended.reshape(item_count, q_width).astype(jnp.bfloat16)
    swap = [(0, 1), (1, 0)]
    sibling_weights = [lax.ppermute(w[0], "c", perm=swap) for w in (expert_gate, expert_up, expert_down)]
    attended, *sibling_weights = lax.optimization_barrier((attended, *sibling_weights))
    pair_gate = jnp.concatenate([expert_gate[0], sibling_weights[0]], axis=1)
    pair_up = jnp.concatenate([expert_up[0], sibling_weights[1]], axis=1)
    pair_down = jnp.concatenate([expert_down[0], sibling_weights[2]], axis=0)
    attn_sum = lax.psum_scatter(
        jnp.dot(attended, w_out, preferred_element_type=jnp.float32).astype(jnp.bfloat16),
        ("y", "c"),
        scatter_dimension=0,
        tiled=True,
    ).astype(jnp.float32)
    residual = (tokens.astype(jnp.float32) + attn_sum).astype(jnp.bfloat16)
    normed2 = rms_norm(residual.astype(jnp.float32), ffn_gain).astype(jnp.bfloat16)
    logits = jnp.dot(normed2, router, preferred_element_type=jnp.float32)
    picked = jnp.take_along_axis(logits, routes, axis=1)
    weights = jax.nn.softmax(picked, axis=-1)
    flat_routes = routes.reshape(-1)
    expert_ids = jnp.arange(EXPERTS, dtype=jnp.int32)
    onehot_route = (flat_routes[:, None] == expert_ids[None, :]).astype(jnp.int32)
    rank = jnp.cumsum(onehot_route, axis=0) - 1
    slot_rank = jnp.sum(onehot_route * rank, axis=1)
    n_y = lax.axis_size("y")
    halves = n_y // (EXPERTS // lax.axis_size("req"))
    chunks = ROWS // CHUNK_ROWS
    pos = (flat_routes[:, None] * halves + jnp.arange(halves, dtype=jnp.int32)[None, :]) * CHUNK_ROWS
    pos = (pos + (slot_rank % CHUNK_ROWS)[:, None]).reshape(tok_rows, TOPK, halves)
    part_of = (slot_rank // CHUNK_ROWS).reshape(tok_rows, TOPK)
    row_ids = jnp.arange(EXPERTS * halves * CHUNK_ROWS, dtype=jnp.int32)
    placed = pos[:, :, :, None] == row_ids[None, None, None, :]

    def expert_slice(rows, gate_w, up_w, down_w):
        flat = rows.reshape(-1, model_width)
        gate = jnp.dot(flat, gate_w, preferred_element_type=jnp.float32)
        up_val = jnp.dot(flat, up_w, preferred_element_type=jnp.float32)
        hidden = ((up_val + 1.0) * gate * jax.nn.sigmoid(1.702 * gate)).astype(jnp.bfloat16)
        return jnp.dot(hidden, down_w, preferred_element_type=jnp.float32).astype(jnp.bfloat16)

    tables, combines, received = [], [], []
    for part in range(chunks):
        match = placed & (part_of == part)[:, :, None, None]
        dispatch_table = jnp.any(match, axis=(1, 2)).T.astype(jnp.bfloat16)
        send_rows = jnp.dot(dispatch_table, normed2, preferred_element_type=jnp.float32).astype(
            jnp.bfloat16
        )
        send_rows = with_layout_constraint(send_rows, Layout(major_to_minor=(0, 1))).reshape(
            EXPERTS * halves, CHUNK_ROWS, model_width
        )
        combines.append(jnp.sum(jnp.where(match, weights[:, :, None, None], 0.0), axis=(1, 2)))
        received.append(
            lax.all_to_all(send_rows, ("req", "y"), split_axis=0, concat_axis=0, tiled=True)
        )
    chip_sums, returned = [], []
    for part in range(chunks):
        rows = received[part]
        if part > 0:
            rows, chip_sums[-1] = lax.optimization_barrier((rows, chip_sums[-1]))
            returned.append(
                lax.all_to_all(chip_sums[-1], ("req", "y"), split_axis=0, concat_axis=0, tiled=True)
            )
        chip_sum = expert_slice(rows, pair_gate, pair_up, pair_down)
        chip_sum = with_layout_constraint(chip_sum, Layout(major_to_minor=(0, 1)))
        chip_sums.append(chip_sum.reshape(rows.shape))
        if part > 0:
            returned[-1], chip_sums[-1] = lax.optimization_barrier((returned[-1], chip_sums[-1]))
    returned.append(
        lax.all_to_all(chip_sums[-1], ("req", "y"), split_axis=0, concat_axis=0, tiled=True)
    )
    moe_sum = residual.astype(jnp.float32)
    for combine, back in zip(combines, returned):
        back = back.reshape(-1, model_width)
        combine_hi = combine.astype(jnp.bfloat16)
        combine_lo = (combine - combine_hi.astype(jnp.float32)).astype(jnp.bfloat16)
        both = jnp.dot(
            jnp.concatenate([combine_hi, combine_lo], axis=0), back, preferred_element_type=jnp.float32
        )
        moe_sum = moe_sum + (both[:tok_rows] + both[tok_rows:])
    return moe_sum.astype(jnp.bfloat16)


def solution(mesh):
    n_req, n_exp = mesh.devices.shape
    fine = jax.sharding.Mesh(mesh.devices.reshape(n_req, n_exp // 2, 2), ("req", "y", "c"))
    tok = ("req", "y", "c")
    return jax.shard_map(
        per_device,
        mesh=fine,
        in_specs=(
            P(tok, None),
            P(),
            P(None, ("y", "c")),
            P(None, ("y", "c")),
            P(None, ("y", "c")),
            P(("y", "c")),
            P(("y", "c"), None),
            P(),
            P(),
            P(tok, None),
            P("req", None),
            P(tok, None, None),
            P(tok, None, None),
            P(tok, None, None),
        ),
        out_specs=P(tok, None),
        check_vma=False,
    )
```

```python
import jax
import jax.numpy as jnp
from jax import lax
from jax.experimental.layout import Layout, with_layout_constraint
from jax.sharding import PartitionSpec as P

QUERY_HEADS = 64
KEY_VALUE_HEADS = 8
HEAD_DIM = 64
EXPERTS = 32
TOPK = 4
CAP = 14
ROWS = 16
CHUNK_ROWS = 8
LONGEST = 384
QUERY_BLOCKS = 6


def rms_norm(value_rows, gain):
    mean_sq = jnp.mean(value_rows * value_rows, axis=-1, keepdims=True)
    return value_rows * lax.rsqrt(mean_sq + 1e-05) * gain


def rotate(value_rows, offset):
    half = value_rows.shape[-1] // 2
    freqs = jnp.exp(
        -(2.0 * jnp.arange(half, dtype=jnp.float32) / value_rows.shape[-1])
        * jnp.log(jnp.float32(150000.0))
    )
    angle = offset.astype(jnp.float32)[:, None] * freqs[None, :]
    cosine = jnp.cos(angle)[:, None, :]
    sine = jnp.sin(angle)[:, None, :]
    first = value_rows[..., :half]
    second = value_rows[..., half:]
    return jnp.concatenate(
        [first * cosine - second * sine, second * cosine + first * sine], axis=-1
    )


def per_device(
    tokens,
    attn_gain,
    w_query,
    key_weight,
    value_weight,
    sinks,
    w_out,
    ffn_gain,
    router,
    routes,
    lengths,
    expert_gate,
    expert_up,
    expert_down,
):
    tok_rows = tokens.shape[0]
    model_width = tokens.shape[1]
    local_heads = w_query.shape[1] // HEAD_DIM
    local_kv = key_weight.shape[1] // HEAD_DIM
    head_group = QUERY_HEADS // KEY_VALUE_HEADS
    normed_input = rms_norm(tokens.astype(jnp.float32), attn_gain).astype(jnp.bfloat16)
    piece = lax.all_gather(normed_input, ("y", "c"), axis=0, tiled=True)
    qkv_weight = jnp.concatenate([w_query, key_weight, value_weight], axis=1)
    projected = jnp.dot(piece, qkv_weight, preferred_element_type=jnp.float32)
    item_count = projected.shape[0]
    lens = lengths[0]
    ends = jnp.cumsum(lens)
    starts = ends - lens
    position = jnp.arange(item_count, dtype=jnp.int32)
    member = ((position[:, None] >= starts[None, :]) & (position[:, None] < ends[None, :])).astype(
        jnp.int32
    )
    segment = jnp.sum(member * jnp.arange(lens.shape[0], dtype=jnp.int32)[None, :], axis=1)
    offset = position - jnp.sum(member * starts[None, :], axis=1)
    q_width = local_heads * HEAD_DIM
    kv_width = local_kv * HEAD_DIM
    query_rows = rotate(
        projected[:, :q_width].reshape(item_count, local_heads, HEAD_DIM), offset
    ).astype(jnp.bfloat16)
    key_rows = rotate(
        projected[:, q_width : q_width + kv_width].reshape(item_count, local_kv, HEAD_DIM), offset
    ).astype(jnp.bfloat16)
    value_rows = (
        projected[:, q_width + kv_width :]
        .reshape(item_count, local_kv, HEAD_DIM)
        .astype(jnp.bfloat16)
    )
    grouped_heads = query_rows.reshape(item_count, local_kv, head_group, HEAD_DIM)
    sink_score_logit = sinks.reshape(local_kv, head_group, 1, 1)
    block = item_count // QUERY_BLOCKS
    edges = [0] + list(range(2 * block, item_count + 1, block))
    pieces = []
    for q0, q1 in zip(edges[:-1], edges[1:]):
        k0 = max(0, (q0 - LONGEST + 1) // block * block)
        scores = jnp.einsum(
            "qcgd,kcd->cgqk", grouped_heads[q0:q1], key_rows[k0:q1], preferred_element_type=jnp.float32
        ) * HEAD_DIM ** (-0.5)
        allowed = (segment[q0:q1, None] == segment[None, k0:q1]) & (
            position[None, k0:q1] <= position[q0:q1, None]
        )
        masked = jnp.where(allowed[None, None], scores, -jnp.inf)
        top = jnp.maximum(jnp.max(masked, axis=-1, keepdims=True), sink_score_logit)
        expo = jnp.where(allowed[None, None], jnp.exp(scores - top), 0.0)
        denom = jnp.sum(expo, axis=-1, keepdims=True) + jnp.exp(sink_score_logit - top)
        probs = (expo / denom).astype(jnp.bfloat16)
        pieces.append(
            jnp.einsum("cgqk,kcd->qcgd", probs, value_rows[k0:q1], preferred_element_type=jnp.float32)
        )
    attended = jnp.concatenate(pieces, axis=0)
    attended = attended.reshape(item_count, q_width).astype(jnp.bfloat16)
    swap = [(0, 1), (1, 0)]
    sibling_weights = [lax.ppermute(w[0], "c", perm=swap) for w in (expert_gate, expert_up, expert_down)]
    attended, *sibling_weights = lax.optimization_barrier((attended, *sibling_weights))
    pair_gate = jnp.concatenate([expert_gate[0], sibling_weights[0]], axis=1)
    pair_up = jnp.concatenate([expert_up[0], sibling_weights[1]], axis=1)
    pair_down = jnp.concatenate([expert_down[0], sibling_weights[2]], axis=0)
    attn_sum = lax.psum_scatter(
        jnp.dot(attended, w_out, preferred_element_type=jnp.float32).astype(jnp.bfloat16),
        ("y", "c"),
        scatter_dimension=0,
        tiled=True,
    ).astype(jnp.float32)
    residual = (tokens.astype(jnp.float32) + attn_sum).astype(jnp.bfloat16)
    normed2 = rms_norm(residual.astype(jnp.float32), ffn_gain).astype(jnp.bfloat16)
    logits = jnp.dot(normed2, router, preferred_element_type=jnp.float32)
    picked = jnp.take_along_axis(logits, routes, axis=1)
    weights = jax.nn.softmax(picked, axis=-1)
    flat_routes = routes.reshape(-1)
    expert_ids = jnp.arange(EXPERTS, dtype=jnp.int32)
    onehot_route = (flat_routes[:, None] == expert_ids[None, :]).astype(jnp.int32)
    rank = jnp.cumsum(onehot_route, axis=0) - 1
    slot_rank = jnp.sum(onehot_route * rank, axis=1)
    n_y = lax.axis_size("y")
    halves = n_y // (EXPERTS // lax.axis_size("req"))
    chunks = ROWS // CHUNK_ROWS
    pos = (flat_routes[:, None] * halves + jnp.arange(halves, dtype=jnp.int32)[None, :]) * CHUNK_ROWS
    pos = (pos + (slot_rank % CHUNK_ROWS)[:, None]).reshape(tok_rows, TOPK, halves)
    part_of = (slot_rank // CHUNK_ROWS).reshape(tok_rows, TOPK)
    row_ids = jnp.arange(EXPERTS * halves * CHUNK_ROWS, dtype=jnp.int32)
    placed = pos[:, :, :, None] == row_ids[None, None, None, :]

    def expert_slice(rows, gate_w, up_w, down_w):
        flat = rows.reshape(-1, model_width)
        gate = jnp.dot(flat, gate_w, preferred_element_type=jnp.float32)
        up_val = jnp.dot(flat, up_w, preferred_element_type=jnp.float32)
        hidden = ((up_val + 1.0) * gate * jax.nn.sigmoid(1.702 * gate)).astype(jnp.bfloat16)
        return jnp.dot(hidden, down_w, preferred_element_type=jnp.float32).astype(jnp.bfloat16)

    tables, combines, received = [], [], []
    for part in range(chunks):
        match = placed & (part_of == part)[:, :, None, None]
        dispatch_table = jnp.any(match, axis=(1, 2)).T.astype(jnp.bfloat16)
        send_rows = jnp.dot(dispatch_table, normed2, preferred_element_type=jnp.float32).astype(
            jnp.bfloat16
        )
        send_rows = with_layout_constraint(send_rows, Layout(major_to_minor=(0, 1))).reshape(
            EXPERTS * halves, CHUNK_ROWS, model_width
        )
        combines.append(jnp.sum(jnp.where(match, weights[:, :, None, None], 0.0), axis=(1, 2)))
        received.append(
            lax.all_to_all(send_rows, ("req", "y"), split_axis=0, concat_axis=0, tiled=True)
        )
    chip_sums, returned = [], []
    for part in range(chunks):
        rows = received[part]
        if part > 0:
            rows, chip_sums[-1] = lax.optimization_barrier((rows, chip_sums[-1]))
            returned.append(
                lax.all_to_all(chip_sums[-1], ("req", "y"), split_axis=0, concat_axis=0, tiled=True)
            )
        chip_sum = expert_slice(rows, pair_gate, pair_up, pair_down)
        chip_sum = with_layout_constraint(chip_sum, Layout(major_to_minor=(0, 1)))
        chip_sums.append(chip_sum.reshape(rows.shape))
        if part > 0:
            returned[-1], chip_sums[-1] = lax.optimization_barrier((returned[-1], chip_sums[-1]))
    returned.append(
        lax.all_to_all(chip_sums[-1], ("req", "y"), split_axis=0, concat_axis=0, tiled=True)
    )
    moe_sum = residual.astype(jnp.float32)
    for combine, back in zip(combines, returned):
        back = back.reshape(-1, model_width)
        combine_hi = combine.astype(jnp.bfloat16)
        combine_lo = (combine - combine_hi.astype(jnp.float32)).astype(jnp.bfloat16)
        both = jnp.dot(
            jnp.concatenate([combine_hi, combine_lo], axis=0), back, preferred_element_type=jnp.float32
        )
        moe_sum = moe_sum + (both[:tok_rows] + both[tok_rows:])
    return moe_sum.astype(jnp.bfloat16)


def solution(mesh):
    n_req, n_exp = mesh.devices.shape
    fine = jax.sharding.Mesh(mesh.devices.reshape(n_req, n_exp // 2, 2), ("req", "y", "c"))
    tok = ("req", "y", "c")
    return jax.shard_map(
        per_device,
        mesh=fine,
        in_specs=(
            P(tok, None),
            P(),
            P(None, ("y", "c")),
            P(None, ("y", "c")),
            P(None, ("y", "c")),
            P(("y", "c")),
            P(("y", "c"), None),
            P(),
            P(),
            P(tok, None),
            P("req", None),
            P(tok, None, None),
            P(tok, None, None),
            P(tok, None, None),
        ),
        out_specs=P(tok, None),
        check_vma=False,
    )
```

```python
import jax
import jax.numpy as jnp
from jax import lax
from jax.experimental.layout import Layout, with_layout_constraint
from jax.sharding import PartitionSpec as P

QUERY_HEADS = 64
KEY_VALUE_HEADS = 8
HEAD_DIM = 64
EXPERTS = 32
TOPK = 4
CAP = 14
ROWS = 16
CHUNK_ROWS = 8
LONGEST = 384
QUERY_BLOCKS = 6


def rms_norm(value_rows, gain):
    mean_sq = jnp.mean(value_rows * value_rows, axis=-1, keepdims=True)
    return value_rows * lax.rsqrt(mean_sq + 1e-05) * gain


def rotate(value_rows, offset):
    half = value_rows.shape[-1] // 2
    freqs = jnp.exp(
        -(2.0 * jnp.arange(half, dtype=jnp.float32) / value_rows.shape[-1])
        * jnp.log(jnp.float32(150000.0))
    )
    angle = offset.astype(jnp.float32)[:, None] * freqs[None, :]
    cosine = jnp.cos(angle)[:, None, :]
    sine = jnp.sin(angle)[:, None, :]
    first = value_rows[..., :half]
    second = value_rows[..., half:]
    return jnp.concatenate(
        [first * cosine - second * sine, second * cosine + first * sine], axis=-1
    )


def per_device(
    tokens,
    attn_gain,
    w_query,
    key_weight,
    value_weight,
    sinks,
    w_out,
    ffn_gain,
    router,
    routes,
    lengths,
    expert_gate,
    expert_up,
    expert_down,
):
    tok_rows = tokens.shape[0]
    model_width = tokens.shape[1]
    local_heads = w_query.shape[1] // HEAD_DIM
    local_kv = key_weight.shape[1] // HEAD_DIM
    head_group = QUERY_HEADS // KEY_VALUE_HEADS
    normed_input = rms_norm(tokens.astype(jnp.float32), attn_gain).astype(jnp.bfloat16)
    piece = lax.all_gather(normed_input, ("y", "c"), axis=0, tiled=True)
    qkv_weight = jnp.concatenate([w_query, key_weight, value_weight], axis=1)
    projected = jnp.dot(piece, qkv_weight, preferred_element_type=jnp.float32)
    item_count = projected.shape[0]
    lens = lengths[0]
    ends = jnp.cumsum(lens)
    starts = ends - lens
    position = jnp.arange(item_count, dtype=jnp.int32)
    member = ((position[:, None] >= starts[None, :]) & (position[:, None] < ends[None, :])).astype(
        jnp.int32
    )
    segment = jnp.sum(member * jnp.arange(lens.shape[0], dtype=jnp.int32)[None, :], axis=1)
    offset = position - jnp.sum(member * starts[None, :], axis=1)
    q_width = local_heads * HEAD_DIM
    kv_width = local_kv * HEAD_DIM
    query_rows = rotate(
        projected[:, :q_width].reshape(item_count, local_heads, HEAD_DIM), offset
    ).astype(jnp.bfloat16)
    key_rows = rotate(
        projected[:, q_width : q_width + kv_width].reshape(item_count, local_kv, HEAD_DIM), offset
    ).astype(jnp.bfloat16)
    value_rows = (
        projected[:, q_width + kv_width :]
        .reshape(item_count, local_kv, HEAD_DIM)
        .astype(jnp.bfloat16)
    )
    grouped_heads = query_rows.reshape(item_count, local_kv, head_group, HEAD_DIM)
    sink_score_logit = sinks.reshape(local_kv, head_group, 1, 1)
    block = item_count // QUERY_BLOCKS
    pieces = []
    for b in range(QUERY_BLOCKS):
        q0, q1 = b * block, (b + 1) * block
        k0 = max(0, (q0 - LONGEST + 1) // block * block)
        scores = jnp.einsum(
            "qcgd,kcd->cgqk", grouped_heads[q0:q1], key_rows[k0:q1], preferred_element_type=jnp.float32
        ) * HEAD_DIM ** (-0.5)
        allowed = (segment[q0:q1, None] == segment[None, k0:q1]) & (
            position[None, k0:q1] <= position[q0:q1, None]
        )
        masked = jnp.where(allowed[None, None], scores, -jnp.inf)
        top = jnp.maximum(jnp.max(masked, axis=-1, keepdims=True), sink_score_logit)
        expo = jnp.where(allowed[None, None], jnp.exp(scores - top), 0.0)
        denom = jnp.sum(expo, axis=-1, keepdims=True) + jnp.exp(sink_score_logit - top)
        probs = (expo * (1.0 / denom)).astype(jnp.bfloat16)
        pieces.append(
            jnp.einsum("cgqk,kcd->qcgd", probs, value_rows[k0:q1], preferred_element_type=jnp.float32)
        )
    attended = jnp.concatenate(pieces, axis=0)
    attended = attended.reshape(item_count, q_width).astype(jnp.bfloat16)
    swap = [(0, 1), (1, 0)]
    sibling_weights = [lax.ppermute(w[0], "c", perm=swap) for w in (expert_gate, expert_up, expert_down)]
    attended, *sibling_weights = lax.optimization_barrier((attended, *sibling_weights))
    pair_gate = jnp.concatenate([expert_gate[0], sibling_weights[0]], axis=1)
    pair_up = jnp.concatenate([expert_up[0], sibling_weights[1]], axis=1)
    pair_down = jnp.concatenate([expert_down[0], sibling_weights[2]], axis=0)
    attn_sum = lax.psum_scatter(
        jnp.dot(attended, w_out, preferred_element_type=jnp.float32).astype(jnp.bfloat16),
        ("y", "c"),
        scatter_dimension=0,
        tiled=True,
    ).astype(jnp.float32)
    residual = (tokens.astype(jnp.float32) + attn_sum).astype(jnp.bfloat16)
    normed2 = rms_norm(residual.astype(jnp.float32), ffn_gain).astype(jnp.bfloat16)
    logits = jnp.dot(normed2, router, preferred_element_type=jnp.float32)
    picked = jnp.take_along_axis(logits, routes, axis=1)
    weights = jax.nn.softmax(picked, axis=-1)
    flat_routes = routes.reshape(-1)
    expert_ids = jnp.arange(EXPERTS, dtype=jnp.int32)
    onehot_route = (flat_routes[:, None] == expert_ids[None, :]).astype(jnp.int32)
    rank = jnp.cumsum(onehot_route, axis=0) - 1
    slot_rank = jnp.sum(onehot_route * rank, axis=1)
    n_y = lax.axis_size("y")
    halves = n_y // (EXPERTS // lax.axis_size("req"))
    chunks = ROWS // CHUNK_ROWS
    pos = (flat_routes[:, None] * halves + jnp.arange(halves, dtype=jnp.int32)[None, :]) * CHUNK_ROWS
    pos = (pos + (slot_rank % CHUNK_ROWS)[:, None]).reshape(tok_rows, TOPK, halves)
    part_of = (slot_rank // CHUNK_ROWS).reshape(tok_rows, TOPK)
    row_ids = jnp.arange(EXPERTS * halves * CHUNK_ROWS, dtype=jnp.int32)
    placed = pos[:, :, :, None] == row_ids[None, None, None, :]

    def expert_slice(rows, gate_w, up_w, down_w):
        flat = rows.reshape(-1, model_width)
        gate = jnp.dot(flat, gate_w, preferred_element_type=jnp.float32)
        up_val = jnp.dot(flat, up_w, preferred_element_type=jnp.float32)
        hidden = ((up_val + 1.0) * gate * jax.nn.sigmoid(1.702 * gate)).astype(jnp.bfloat16)
        return jnp.dot(hidden, down_w, preferred_element_type=jnp.float32).astype(jnp.bfloat16)

    tables, combines, received = [], [], []
    for part in range(chunks):
        match = placed & (part_of == part)[:, :, None, None]
        dispatch_table = jnp.any(match, axis=(1, 2)).T.astype(jnp.bfloat16)
        send_rows = jnp.dot(dispatch_table, normed2, preferred_element_type=jnp.float32).astype(
            jnp.bfloat16
        )
        send_rows = with_layout_constraint(send_rows, Layout(major_to_minor=(0, 1))).reshape(
            EXPERTS * halves, CHUNK_ROWS, model_width
        )
        combines.append(jnp.sum(jnp.where(match, weights[:, :, None, None], 0.0), axis=(1, 2)))
        received.append(
            lax.all_to_all(send_rows, ("req", "y"), split_axis=0, concat_axis=0, tiled=True)
        )
    chip_sums, returned = [], []
    for part in range(chunks):
        rows = received[part]
        if part > 0:
            rows, chip_sums[-1] = lax.optimization_barrier((rows, chip_sums[-1]))
            returned.append(
                lax.all_to_all(chip_sums[-1], ("req", "y"), split_axis=0, concat_axis=0, tiled=True)
            )
        chip_sum = expert_slice(rows, pair_gate, pair_up, pair_down)
        chip_sum = with_layout_constraint(chip_sum, Layout(major_to_minor=(0, 1)))
        chip_sums.append(chip_sum.reshape(rows.shape))
        if part > 0:
            returned[-1], chip_sums[-1] = lax.optimization_barrier((returned[-1], chip_sums[-1]))
    returned.append(
        lax.all_to_all(chip_sums[-1], ("req", "y"), split_axis=0, concat_axis=0, tiled=True)
    )
    moe_sum = residual.astype(jnp.float32)
    for combine, back in zip(combines, returned):
        back = back.reshape(-1, model_width)
        combine_hi = combine.astype(jnp.bfloat16)
        combine_lo = (combine - combine_hi.astype(jnp.float32)).astype(jnp.bfloat16)
        both = jnp.dot(
            jnp.concatenate([combine_hi, combine_lo], axis=0), back, preferred_element_type=jnp.float32
        )
        moe_sum = moe_sum + (both[:tok_rows] + both[tok_rows:])
    return moe_sum.astype(jnp.bfloat16)


def solution(mesh):
    n_req, n_exp = mesh.devices.shape
    fine = jax.sharding.Mesh(mesh.devices.reshape(n_req, n_exp // 2, 2), ("req", "y", "c"))
    tok = ("req", "y", "c")
    return jax.shard_map(
        per_device,
        mesh=fine,
        in_specs=(
            P(tok, None),
            P(),
            P(None, ("y", "c")),
            P(None, ("y", "c")),
            P(None, ("y", "c")),
            P(("y", "c")),
            P(("y", "c"), None),
            P(),
            P(),
            P(tok, None),
            P("req", None),
            P(tok, None, None),
            P(tok, None, None),
            P(tok, None, None),
        ),
        out_specs=P(tok, None),
        check_vma=False,
    )
```
